128 devices in a mesh: dev: 128 (over x, y, z, core).
Axes of the slice: x: 4, y: 4, z: 4, core: 2. Of those that a mesh axis runs over, the one named last changes fastest.
Arguments:
- right_sides: float32 [128, 256, 512], P('dev'), may hold values from -6 to 6
- diag_inverse: float32 [256, 512, 512], P('dev'), may hold values from -0.25 to 0.25
- factor_tiles: float32 [1024, 512, 512], P('dev'), may hold values from -0.09375 to 0.09375
- node_level: int32 [256], replicated, may hold values from 0 to 4, as said below
- tile_column: int32 [1024], replicated, may hold values from 0 to 255, as said below
- tile_row: int32 [1024], replicated, may hold values from 0 to 255, as said below
Outputs:
- solution: float32 [128, 256, 512], P('dev')
The draws below stay inside these ranges and needn't reach their ends.
Inputs may be any that keep to these rules, and one draw needn't show every extreme that they name: `node_level`: supernode s is owned by device s // 2; the 2 supernodes of one device lie at different levels, and every level holds supernodes of two or more devices. `tile_column`: tile k is held by device k // 8; its column supernode lies at a lower level than its row supernode. Among one device's tiles whose column supernodes lie at one level there are at most 4 tiles, 2 distinct column supernodes and 2 distinct row supernodes; some device reaches all three bounds. A pair of supernodes may recur on several tiles. `tile_row`: drawn together with tile_column, under its bounds.
All inputs are finite; a program needn't handle non-finite values.
Results may differ from the reference program's by a relative error of at most 0.0001.
Values sent between devices are 32-bit elements; how exact they have to be, the bound alone decides.
No kernel may reach another device: no remote copies, remote signals or barrier semaphores. Data moves between devices by JAX's collectives and lax.ppermute only.
A program may use at most 128 MiB of HBM per device.

```python
import jax
import jax.numpy as jnp
from jax import lax

B = 512
SN_DEV = 2
TILE_DEV = 8
LEVELS = 5
R = 128
NS = 256
NT = 1024


def build_tables(key):
    owners = NS // SN_DEV
    first_level = jnp.arange(owners, dtype=jnp.int32) % LEVELS
    advance = jax.random.randint(jax.random.fold_in(key, 101), (owners,), 1, LEVELS)
    second_level = (first_level + advance) % LEVELS
    node_level = jnp.stack([first_level, second_level], axis=1).reshape(-1).astype(jnp.int32)
    pattern = jax.random.randint(jax.random.fold_in(key, 102), (owners,), 0, 2)
    pattern = pattern.at[0].set(0)
    scores = jax.random.randint(jax.random.fold_in(key, 103), (owners, 4), 0, 1 << 20) * 4 + jnp.arange(4, dtype=jnp.int32)
    ranking = jnp.argsort(scores, axis=1, stable=True)
    base_counts = jnp.array([4, 2, 1, 1], dtype=jnp.int32)
    counts = jnp.where(pattern[:, None] == 0, base_counts[ranking], 2)
    end_slot = jnp.cumsum(counts, axis=1)
    start_slot = end_slot - counts
    slot_ids = jnp.arange(TILE_DEV, dtype=jnp.int32)
    group_level = jnp.sum((slot_ids[None, :, None] >= end_slot[:, None, :]).astype(jnp.int32), axis=2)
    group_start = jnp.take_along_axis(start_slot, group_level, axis=1)
    within_group = slot_ids[None, :] - group_start
    level_ids = jnp.arange(4, dtype=jnp.int32)
    node_ids = jnp.arange(NS, dtype=jnp.int32)

    def choose_two(salt_value, allowed):
        picks = jax.random.randint(jax.random.fold_in(key, salt_value), (owners, 4, NS), 0, 1 << 20) * NS + node_ids
        picks = jnp.where(allowed[None, :, :], picks, -1)
        return lax.top_k(picks, 2)[1].astype(jnp.int32)
    column_picks = choose_two(104, node_level[None, :] == level_ids[:, None])
    row_picks = choose_two(105, node_level[None, :] > level_ids[:, None])
    column = jnp.take_along_axis(column_picks.reshape(owners, 8), group_level * 2 + within_group % 2, axis=1)
    row = jnp.take_along_axis(row_picks.reshape(owners, 8), group_level * 2 + within_group // 2, axis=1)
    return (node_level, column.reshape(-1).astype(jnp.int32), row.reshape(-1).astype(jnp.int32))


def draw_node_level(key, part):
    return build_tables(key)[0]


def draw_tile_column(key, part):
    return build_tables(key)[1]


def draw_tile_row(key, part):
    return build_tables(key)[2]


def levels(own_key, dims, pieces, least, largest):
    factor_of, own = 1.0, jax.random.fold_in(own_key, 6)
    for axis_at, parts in pieces:
        draws = jnp.exp(jax.random.uniform(jax.random.fold_in(own, axis_at), (parts,), jnp.float32, least / len(pieces), largest / len(pieces)))
        factor_of = factor_of * jnp.repeat(draws, dims[axis_at] // parts).reshape([-1 if axis == axis_at else 1 for axis in range(len(dims))])
    return factor_of


def gaussian(rng, dims, spread, bound, cuts=(), held_as=jnp.bfloat16):
    drawn = spread * jax.random.normal(rng, dims, jnp.float32)
    if cuts:
        drawn = drawn * levels(rng, dims, cuts, -0.22, 0.18)
    return jnp.clip(drawn, -bound, bound).astype(held_as)


def setup_inputs(seed: int = 0) -> dict:
    keys = jax.random.split(jax.random.key(seed), 7)
    right_sides = gaussian(keys[0], (R, NS, B), 1.0, 6.0, ((0, 128),), jnp.float32)
    diag_inverse = gaussian(keys[1], (NS, B, B), B ** -0.5, 0.25, ((0, 128),), jnp.float32)
    factor_tiles = gaussian(keys[2], (NT, B, B), (8 * B) ** -0.5, 0.09375, ((0, 128),), jnp.float32)
    node_level = draw_node_level(jax.random.fold_in(keys[6], 71), 0)
    tile_column = draw_tile_column(jax.random.fold_in(keys[6], 71), 0)
    tile_row = draw_tile_row(jax.random.fold_in(keys[6], 71), 0)
    return dict(right_sides=right_sides, diag_inverse=diag_inverse, factor_tiles=factor_tiles, node_level=node_level, tile_column=tile_column, tile_row=tile_row)


full_precision = lax.Precision.HIGHEST


def reference(right_sides, diag_inverse, factor_tiles, node_level, tile_column, tile_row):
    tile_level = node_level[tile_column].astype(jnp.int32)
    ranking = jnp.argsort(tile_level, stable=True).astype(jnp.int32)
    solution = jnp.zeros_like(right_sides)
    update = jnp.zeros_like(right_sides)
    for current in range(LEVELS):
        solved = jnp.einsum('rsb,sbc->rsc', right_sides - update, diag_inverse, precision=full_precision)
        chosen = (node_level == current)[None, :, None]
        solution = jnp.where(chosen, solved, solution)
        first_tile = jnp.sum((tile_level < current).astype(jnp.int32)).astype(jnp.int32)
        last_tile = jnp.sum((tile_level <= current).astype(jnp.int32)).astype(jnp.int32)

        def apply_tile(position, partial_value, known=solution):
            tile_id = ranking[position]
            source = lax.dynamic_index_in_dim(known, tile_column[tile_id], 1, keepdims=False)
            term = jnp.dot(source, factor_tiles[tile_id], precision=full_precision, preferred_element_type=jnp.float32)
            target = lax.dynamic_index_in_dim(partial_value, tile_row[tile_id], 1, keepdims=False)
            return lax.dynamic_update_index_in_dim(partial_value, target + term, tile_row[tile_id], 1)

        update = lax.fori_loop(first_tile, last_tile, apply_tile, update)
    return solution
```

```python
import jax
import jax.numpy as jnp
from jax import lax
from jax.sharding import PartitionSpec as P

LEVELS = 5
ACTIVE = 4

product_precision = lax.Precision.HIGH
select_precision = lax.Precision.HIGHEST


def first_true(mask):
    return jnp.argmax(mask, axis=-1).astype(jnp.int32), jnp.any(mask, axis=-1)


def two_distinct(labels, active):
    i0, v0 = first_true(active)
    l0 = jnp.take_along_axis(labels, i0[:, None], axis=1)[:, 0]
    other = active & (labels != l0[:, None])
    i1, v1 = first_true(other)
    l1 = jnp.take_along_axis(labels, i1[:, None], axis=1)[:, 0]
    slot = jnp.where(labels == l0[:, None], 0, 1).astype(jnp.int32)
    return jnp.stack([l0, l1], axis=1), jnp.stack([v0, v1], axis=1), slot


def a2a(x):
    return lax.all_to_all(x, "dev", split_axis=0, concat_axis=0, tiled=True)


def per_device(right_sides, diag_inverse, factor_tiles, node_level, tile_column, tile_row):
    devices = lax.axis_size("dev")
    myself = lax.axis_index("dev")
    per_owner = diag_inverse.shape[0]
    per_holder = factor_tiles.shape[0]
    block = factor_tiles.shape[1]
    supernodes = node_level.shape[0]

    rhs = right_sides[0].reshape(devices, per_owner, block)
    update = jnp.zeros_like(rhs)
    solution = jnp.zeros_like(rhs)

    owner_levels = node_level.reshape(devices, per_owner)
    tile_level = jnp.take(node_level, tile_column, axis=0)
    holder_levels = tile_level.reshape(devices, per_holder)
    holder_columns = tile_column.reshape(devices, per_holder)
    holder_rows = tile_row.reshape(devices, per_holder)
    node_ids = jnp.arange(supernodes, dtype=jnp.int32)

    for current in range(LEVELS):
        at_level = owner_levels == current
        has_one = jnp.any(at_level, axis=1)
        slot_of = jnp.argmax(at_level, axis=1).astype(jnp.int32)
        pick = (slot_of[:, None] == jnp.arange(per_owner, dtype=jnp.int32)[None, :])[:, :, None]

        residue = jnp.sum(jnp.where(pick, rhs - update, 0.0), axis=1)
        gathered = a2a(residue)
        my_slot = slot_of[myself]
        inverse = lax.dynamic_index_in_dim(diag_inverse, my_slot, 0, keepdims=False)
        solved = jnp.dot(gathered, inverse, precision=product_precision,
                         preferred_element_type=jnp.float32)
        returned = a2a(solved)
        solution = jnp.where(pick & has_one[:, None, None], returned[:, None, :], solution)

        if current + 1 < LEVELS:
            active = holder_levels == current
            col_ids, col_valid, col_slot = two_distinct(holder_columns, active)
            row_ids, row_valid, row_slot = two_distinct(holder_rows, active)

            flat = solution.reshape(supernodes, block)
            carried = jnp.take(flat, col_ids.reshape(-1), axis=0).reshape(devices, 2, block)
            blocks = a2a(carried)

            mine_active = active[myself]
            mine_col_slot = col_slot[myself]
            mine_row_slot = row_slot[myself]
            order = jnp.cumsum(mine_active.astype(jnp.int32)) - 1
            sums = [jnp.zeros((blocks.shape[0], block), jnp.float32) for _ in range(2)]
            for t in range(ACTIVE):
                hit = mine_active & (order == t)
                tile = jnp.argmax(hit).astype(jnp.int32)
                present = jnp.any(hit)
                cs = mine_col_slot[tile]
                rs = mine_row_slot[tile]
                source = lax.dynamic_index_in_dim(blocks, cs, 1, keepdims=False)
                factor = lax.dynamic_index_in_dim(factor_tiles, tile, 0, keepdims=False)
                term = jnp.dot(source, factor, precision=product_precision,
                               preferred_element_type=jnp.float32)
                for j in range(2):
                    sums[j] = sums[j] + jnp.where(present & (rs == j), term, 0.0)
            products = jnp.stack(sums, axis=1)
            coming = a2a(products).reshape(devices * 2, block)

            targets = jnp.where(row_valid, row_ids, -1).reshape(-1)
            onehot = (node_ids[:, None] == targets[None, :]).astype(jnp.float32)
            added = jnp.dot(onehot, coming, precision=select_precision,
                            preferred_element_type=jnp.float32)
            update = update + added.reshape(devices, per_owner, block)
    return solution.reshape(1, supernodes, block)


def solution(mesh):
    placed = (P("dev", None, None), P("dev", None, None), P("dev", None, None), P(), P(), P())
    return jax.shard_map(
        per_device, mesh=mesh, in_specs=placed, out_specs=P("dev", None, None), check_vma=False
    )
```

```python
import jax
import jax.numpy as jnp
from jax import lax
from jax.sharding import PartitionSpec as P

LEVELS = 5
ACTIVE = 4

product_precision = lax.Precision.HIGH
select_precision = lax.Precision.HIGHEST


def first_mask(mask):
    return mask & (jnp.cumsum(mask.astype(jnp.int32), axis=-1) == 1)


def two_distinct(labels, active):
    l0 = jnp.sum(jnp.where(first_mask(active), labels[None], 0), axis=-1)
    other = active & (labels[None] != l0[..., None])
    l1 = jnp.sum(jnp.where(first_mask(other), labels[None], 0), axis=-1)
    ids = jnp.stack([l0, l1], axis=-1)
    valid = jnp.stack([jnp.any(active, axis=-1), jnp.any(other, axis=-1)], axis=-1)
    slot = (labels[None] != l0[..., None]).astype(jnp.int32)
    return ids, valid, slot


def a2a(x):
    return lax.all_to_all(x, "dev", split_axis=0, concat_axis=0, tiled=True)


def per_device(right_sides, diag_inverse, factor_tiles, node_level, tile_column, tile_row):
    devices = lax.axis_size("dev")
    myself = lax.axis_index("dev")
    per_owner = diag_inverse.shape[0]
    per_holder = factor_tiles.shape[0]
    block = factor_tiles.shape[1]
    supernodes = node_level.shape[0]
    tile_levels = LEVELS - 1

    rhs = right_sides[0].reshape(devices, per_owner, block)
    update = jnp.zeros_like(rhs)
    solution = jnp.zeros_like(rhs)

    node_ids = jnp.arange(supernodes, dtype=jnp.int32)
    level_ids = jnp.arange(LEVELS, dtype=jnp.int32)
    tile_level = jnp.sum(jnp.where(tile_column[:, None] == node_ids[None, :], node_level[None, :], 0), axis=1)
    owner_levels = node_level.reshape(devices, per_owner)
    owner_at = owner_levels[None] == level_ids[:, None, None]
    owner_has = jnp.any(owner_at, axis=-1)
    owner_pick = owner_at & owner_has[..., None]
    my_owner_at = lax.dynamic_index_in_dim(owner_at, myself, 1, keepdims=False)
    my_slot = jnp.sum(jnp.where(my_owner_at, jnp.arange(per_owner, dtype=jnp.int32)[None], 0), axis=-1)

    holder_levels = tile_level.reshape(devices, per_holder)
    active = holder_levels[None] == level_ids[:tile_levels, None, None]
    col_ids, col_valid, col_slot = two_distinct(tile_column.reshape(devices, per_holder), active)
    row_ids, row_valid, row_slot = two_distinct(tile_row.reshape(devices, per_holder), active)
    targets = jnp.where(row_valid, row_ids, -1).reshape(tile_levels, devices * 2)

    mine = lax.dynamic_index_in_dim(active, myself, 1, keepdims=False)
    mine_cs = lax.dynamic_index_in_dim(col_slot, myself, 1, keepdims=False)
    mine_rs = lax.dynamic_index_in_dim(row_slot, myself, 1, keepdims=False)
    order = jnp.cumsum(mine.astype(jnp.int32), axis=-1) - 1
    hit = mine[:, None, :] & (order[:, None, :] == jnp.arange(ACTIVE, dtype=jnp.int32)[None, :, None])
    present = jnp.any(hit, axis=-1)
    tile_ids = jnp.arange(per_holder, dtype=jnp.int32)
    slot_tile = jnp.sum(jnp.where(hit, tile_ids[None, None, :], 0), axis=-1)
    slot_cs = jnp.sum(jnp.where(hit, mine_cs[:, None, :], 0), axis=-1)
    slot_rs = jnp.sum(jnp.where(hit, mine_rs[:, None, :], 0), axis=-1)
    row_mask = present[..., None] & (slot_rs[..., None] == jnp.arange(2, dtype=jnp.int32))

    for current in range(LEVELS):
        pick = owner_pick[current][:, :, None]
        residue = jnp.sum(jnp.where(owner_at[current][:, :, None], rhs - update, 0.0), axis=1)
        gathered = a2a(residue)
        inverse = lax.dynamic_index_in_dim(diag_inverse, my_slot[current], 0, keepdims=False)
        solved = jnp.dot(gathered, inverse, precision=product_precision,
                         preferred_element_type=jnp.float32)
        returned = a2a(solved)
        solution = jnp.where(pick, returned[:, None, :], solution)

        if current < tile_levels:
            flat = solution.reshape(supernodes, block)
            carried = jnp.take(flat, col_ids[current].reshape(-1), axis=0).reshape(devices, 2, block)
            blocks = a2a(carried)

            factors = jnp.take(factor_tiles, slot_tile[current], axis=0)
            sources = jnp.take(blocks, slot_cs[current], axis=1)
            terms = jnp.einsum("rtb,tbc->rtc", sources, factors, precision=product_precision,
                               preferred_element_type=jnp.float32)
            mask = row_mask[current]
            products = jnp.stack(
                [jnp.sum(jnp.where(mask[None, :, j, None], terms, 0.0), axis=1) for j in range(2)], axis=1)
            coming = a2a(products).reshape(devices * 2, block)

            onehot = (node_ids[:, None] == targets[current][None, :]).astype(jnp.float32)
            added = jnp.dot(onehot, coming, precision=select_precision,
                            preferred_element_type=jnp.float32)
            update = update + added.reshape(devices, per_owner, block)
    return solution.reshape(1, supernodes, block)


def solution(mesh):
    placed = (P("dev", None, None), P("dev", None, None), P("dev", None, None), P(), P(), P())
    return jax.shard_map(
        per_device, mesh=mesh, in_specs=placed, out_specs=P("dev", None, None), check_vma=False
    )
```

```python
import jax
import jax.numpy as jnp
from jax import lax
from jax.sharding import PartitionSpec as P

LEVELS = 5
ACTIVE = 4

product_precision = lax.Precision.HIGH
select_precision = lax.Precision.HIGHEST


def prefix_count(mask):
    m = mask.shape[-1]
    upto = jnp.arange(m)[:, None] <= jnp.arange(m)[None, :]
    return jnp.sum((upto & mask[..., :, None]).astype(jnp.int32), axis=-2)


def first_mask(mask):
    return mask & (prefix_count(mask) == 1)


def two_distinct(labels, active):
    l0 = jnp.sum(jnp.where(first_mask(active), labels[None], 0), axis=-1)
    other = active & (labels[None] != l0[..., None])
    l1 = jnp.sum(jnp.where(first_mask(other), labels[None], 0), axis=-1)
    ids = jnp.stack([l0, l1], axis=-1)
    valid = jnp.stack([jnp.any(active, axis=-1), jnp.any(other, axis=-1)], axis=-1)
    slot = (labels[None] != l0[..., None]).astype(jnp.int32)
    return ids, valid, slot


def a2a(x):
    return lax.all_to_all(x, "dev", split_axis=0, concat_axis=0, tiled=True)


def per_device(right_sides, diag_inverse, factor_tiles, node_level, tile_column, tile_row):
    devices = lax.axis_size("dev")
    myself = lax.axis_index("dev")
    per_owner = diag_inverse.shape[0]
    per_holder = factor_tiles.shape[0]
    block = factor_tiles.shape[1]
    supernodes = node_level.shape[0]
    tile_levels = LEVELS - 1

    rhs = right_sides[0].reshape(devices, per_owner, block)
    update = jnp.zeros_like(rhs)
    solution = jnp.zeros_like(rhs)

    node_ids = jnp.arange(supernodes, dtype=jnp.int32)
    level_ids = jnp.arange(LEVELS, dtype=jnp.int32)
    tile_level = jnp.sum(jnp.where(tile_column[:, None] == node_ids[None, :], node_level[None, :], 0), axis=1)
    owner_levels = node_level.reshape(devices, per_owner)
    owner_at = owner_levels[None] == level_ids[:, None, None]
    owner_has = jnp.any(owner_at, axis=-1)
    owner_pick = owner_at & owner_has[..., None]
    my_owner_at = lax.dynamic_index_in_dim(owner_at, myself, 1, keepdims=False)
    my_slot = jnp.sum(jnp.where(my_owner_at, jnp.arange(per_owner, dtype=jnp.int32)[None], 0), axis=-1)

    holder_levels = tile_level.reshape(devices, per_holder)
    active = holder_levels[None] == level_ids[:tile_levels, None, None]
    col_ids, col_valid, col_slot = two_distinct(tile_column.reshape(devices, per_holder), active)
    row_ids, row_valid, row_slot = two_distinct(tile_row.reshape(devices, per_holder), active)
    targets = jnp.where(row_valid, row_ids, -1).reshape(tile_levels, devices * 2)

    mine = lax.dynamic_index_in_dim(active, myself, 1, keepdims=False)
    mine_cs = lax.dynamic_index_in_dim(col_slot, myself, 1, keepdims=False)
    mine_rs = lax.dynamic_index_in_dim(row_slot, myself, 1, keepdims=False)
    order = prefix_count(mine) - 1
    hit = mine[:, None, :] & (order[:, None, :] == jnp.arange(ACTIVE, dtype=jnp.int32)[None, :, None])
    present = jnp.any(hit, axis=-1)
    tile_ids = jnp.arange(per_holder, dtype=jnp.int32)
    slot_tile = jnp.sum(jnp.where(hit, tile_ids[None, None, :], 0), axis=-1)
    slot_cs = jnp.sum(jnp.where(hit, mine_cs[:, None, :], 0), axis=-1)
    slot_rs = jnp.sum(jnp.where(hit, mine_rs[:, None, :], 0), axis=-1)
    row_mask = present[..., None] & (slot_rs[..., None] == jnp.arange(2, dtype=jnp.int32))

    for current in range(LEVELS):
        pick = owner_pick[current][:, :, None]
        residue = jnp.sum(jnp.where(owner_at[current][:, :, None], rhs - update, 0.0), axis=1)
        gathered = a2a(residue)
        inverse = lax.dynamic_index_in_dim(diag_inverse, my_slot[current], 0, keepdims=False)
        solved = jnp.dot(gathered, inverse, precision=product_precision,
                         preferred_element_type=jnp.float32)
        returned = a2a(solved)
        solution = jnp.where(pick, returned[:, None, :], solution)

        if current < tile_levels:
            flat = solution.reshape(supernodes, block)
            carried = jnp.take(flat, col_ids[current].reshape(-1), axis=0).reshape(devices, 2, block)
            blocks = a2a(carried)

            factors = jnp.take(factor_tiles, slot_tile[current], axis=0)
            sources = jnp.take(blocks, slot_cs[current], axis=1)
            terms = jnp.einsum("rtb,tbc->rtc", sources, factors, precision=product_precision,
                               preferred_element_type=jnp.float32)
            mask = row_mask[current]
            products = jnp.stack(
                [jnp.sum(jnp.where(mask[None, :, j, None], terms, 0.0), axis=1) for j in range(2)], axis=1)
            coming = a2a(products).reshape(devices * 2, block)

            onehot = (node_ids[:, None] == targets[current][None, :]).astype(jnp.float32)
            added = jnp.dot(onehot, coming, precision=select_precision,
                            preferred_element_type=jnp.float32)
            update = update + added.reshape(devices, per_owner, block)
    return solution.reshape(1, supernodes, block)


def solution(mesh):
    placed = (P("dev", None, None), P("dev", None, None), P("dev", None, None), P(), P(), P())
    return jax.shard_map(
        per_device, mesh=mesh, in_specs=placed, out_specs=P("dev", None, None), check_vma=False
    )
```

```python
import jax
import jax.numpy as jnp
from jax import lax
from jax.sharding import PartitionSpec as P

LEVELS = 5
ACTIVE = 4

product_precision = lax.Precision.HIGH
select_precision = lax.Precision.HIGHEST


def prefix_count(mask):
    m = mask.shape[-1]
    upto = jnp.arange(m)[:, None] <= jnp.arange(m)[None, :]
    return jnp.sum((upto & mask[..., :, None]).astype(jnp.int32), axis=-2)


def first_mask(mask):
    return mask & (prefix_count(mask) == 1)


def two_distinct(labels, active):
    l0 = jnp.sum(jnp.where(first_mask(active), labels[None], 0), axis=-1)
    other = active & (labels[None] != l0[..., None])
    l1 = jnp.sum(jnp.where(first_mask(other), labels[None], 0), axis=-1)
    ids = jnp.stack([l0, l1], axis=-1)
    valid = jnp.stack([jnp.any(active, axis=-1), jnp.any(other, axis=-1)], axis=-1)
    slot = (labels[None] != l0[..., None]).astype(jnp.int32)
    return ids, valid, slot


def a2a(x):
    return lax.all_to_all(x, "dev", split_axis=0, concat_axis=0, tiled=True)


def per_device(right_sides, diag_inverse, factor_tiles, node_level, tile_column, tile_row):
    devices = lax.axis_size("dev")
    myself = lax.axis_index("dev")
    per_owner = diag_inverse.shape[0]
    per_holder = factor_tiles.shape[0]
    block = factor_tiles.shape[1]
    supernodes = node_level.shape[0]
    tile_levels = LEVELS - 1

    rhs = right_sides[0].reshape(devices, per_owner, block)
    update = jnp.zeros_like(rhs)

    node_ids = jnp.arange(supernodes, dtype=jnp.int32)
    level_ids = jnp.arange(LEVELS, dtype=jnp.int32)
    tile_level = jnp.sum(jnp.where(tile_column[:, None] == node_ids[None, :], node_level[None, :], 0), axis=1)
    owner_levels = node_level.reshape(devices, per_owner)
    owner_at = owner_levels[None] == level_ids[:, None, None]
    my_owner_at = lax.dynamic_index_in_dim(owner_at, myself, 1, keepdims=False)
    my_slot = jnp.sum(jnp.where(my_owner_at, jnp.arange(per_owner, dtype=jnp.int32)[None], 0), axis=-1)

    holder_levels = tile_level.reshape(devices, per_holder)
    active = holder_levels[None] == level_ids[:tile_levels, None, None]
    col_ids, col_valid, col_slot = two_distinct(tile_column.reshape(devices, per_holder), active)
    row_ids, row_valid, row_slot = two_distinct(tile_row.reshape(devices, per_holder), active)
    targets = jnp.where(row_valid, row_ids, -1).reshape(tile_levels, devices * 2)
    col_owner = col_ids // per_owner

    mine = lax.dynamic_index_in_dim(active, myself, 1, keepdims=False)
    mine_cs = lax.dynamic_index_in_dim(col_slot, myself, 1, keepdims=False)
    mine_rs = lax.dynamic_index_in_dim(row_slot, myself, 1, keepdims=False)
    order = prefix_count(mine) - 1
    hit = mine[:, None, :] & (order[:, None, :] == jnp.arange(ACTIVE, dtype=jnp.int32)[None, :, None])
    present = jnp.any(hit, axis=-1)
    tile_ids = jnp.arange(per_holder, dtype=jnp.int32)
    slot_tile = jnp.sum(jnp.where(hit, tile_ids[None, None, :], 0), axis=-1)
    slot_cs = jnp.sum(jnp.where(hit, mine_cs[:, None, :], 0), axis=-1)
    slot_rs = jnp.sum(jnp.where(hit, mine_rs[:, None, :], 0), axis=-1)
    row_mask = present[..., None] & (slot_rs[..., None] == jnp.arange(2, dtype=jnp.int32))

    solved_rows = []
    for current in range(LEVELS):
        residue = jnp.sum(jnp.where(owner_at[current][:, :, None], rhs - update, 0.0), axis=1)
        gathered = a2a(residue)
        inverse = lax.dynamic_index_in_dim(diag_inverse, my_slot[current], 0, keepdims=False)
        solved = jnp.dot(gathered, inverse, precision=product_precision,
                         preferred_element_type=jnp.float32)
        returned = a2a(solved)
        solved_rows.append(returned)

        if current < tile_levels:
            carried = jnp.take(returned, col_owner[current].reshape(-1), axis=0,
                               mode="clip").reshape(devices, 2, block)
            blocks = a2a(carried)

            factors = jnp.take(factor_tiles, slot_tile[current], axis=0, mode="clip")
            sources = jnp.take(blocks, slot_cs[current], axis=1, mode="clip")
            terms = jnp.einsum("rtb,tbc->rtc", sources, factors, precision=product_precision,
                               preferred_element_type=jnp.float32)
            mask = row_mask[current]
            products = jnp.stack(
                [jnp.sum(jnp.where(mask[None, :, j, None], terms, 0.0), axis=1) for j in range(2)], axis=1)
            coming = a2a(products).reshape(devices * 2, block)

            onehot = (node_ids[:, None] == targets[current][None, :]).astype(jnp.float32)
            added = jnp.dot(onehot, coming, precision=select_precision,
                            preferred_element_type=jnp.float32)
            update = update + added.reshape(devices, per_owner, block)
    solution = solved_rows[0][:, None, :]
    for current in range(1, LEVELS):
        solution = jnp.where(owner_at[current][:, :, None], solved_rows[current][:, None, :], solution)
    return solution.reshape(1, supernodes, block)


def solution(mesh):
    placed = (P("dev", None, None), P("dev", None, None), P("dev", None, None), P(), P(), P())
    return jax.shard_map(
        per_device, mesh=mesh, in_specs=placed, out_specs=P("dev", None, None), check_vma=False
    )
```

```python
import jax
import jax.numpy as jnp
from jax import lax
from jax.sharding import PartitionSpec as P

LEVELS = 5
ACTIVE = 4

product_precision = lax.Precision.HIGH
select_precision = lax.Precision.HIGHEST


def prefix_count(mask):
    m = mask.shape[-1]
    upto = jnp.arange(m)[:, None] <= jnp.arange(m)[None, :]
    return jnp.sum((upto & mask[..., :, None]).astype(jnp.int32), axis=-2)


def first_mask(mask):
    return mask & (prefix_count(mask) == 1)


def two_distinct(labels, active):
    l0 = jnp.sum(jnp.where(first_mask(active), labels[None], 0), axis=-1)
    other = active & (labels[None] != l0[..., None])
    l1 = jnp.sum(jnp.where(first_mask(other), labels[None], 0), axis=-1)
    ids = jnp.stack([l0, l1], axis=-1)
    valid = jnp.stack([jnp.any(active, axis=-1), jnp.any(other, axis=-1)], axis=-1)
    slot = (labels[None] != l0[..., None]).astype(jnp.int32)
    return ids, valid, slot


def a2a(x):
    return lax.all_to_all(x, "dev", split_axis=0, concat_axis=0, tiled=True)


def per_device(right_sides, diag_inverse, factor_tiles, node_level, tile_column, tile_row):
    devices = lax.axis_size("dev")
    myself = lax.axis_index("dev")
    per_owner = diag_inverse.shape[0]
    per_holder = factor_tiles.shape[0]
    block = factor_tiles.shape[1]
    supernodes = node_level.shape[0]
    tile_levels = LEVELS - 1

    rhs = right_sides[0].reshape(devices, per_owner, block)
    update = jnp.zeros_like(rhs)

    node_ids = jnp.arange(supernodes, dtype=jnp.int32)
    level_ids = jnp.arange(LEVELS, dtype=jnp.int32)
    tile_level = jnp.sum(jnp.where(tile_column[:, None] == node_ids[None, :], node_level[None, :], 0), axis=1)
    owner_levels = node_level.reshape(devices, per_owner)
    owner_at = owner_levels[None] == level_ids[:, None, None]
    my_owner_at = lax.dynamic_index_in_dim(owner_at, myself, 1, keepdims=False)
    my_slot = jnp.sum(jnp.where(my_owner_at, jnp.arange(per_owner, dtype=jnp.int32)[None], 0), axis=-1)
    owner_slot = jnp.sum(jnp.where(owner_at, jnp.arange(per_owner, dtype=jnp.int32)[None, None], 0), axis=-1)

    holder_levels = tile_level.reshape(devices, per_holder)
    active = holder_levels[None] == level_ids[:tile_levels, None, None]
    col_ids, col_valid, col_slot = two_distinct(tile_column.reshape(devices, per_holder), active)
    row_ids, row_valid, row_slot = two_distinct(tile_row.reshape(devices, per_holder), active)
    targets = jnp.where(row_valid, row_ids, -1).reshape(tile_levels, devices * 2)
    col_owner = col_ids // per_owner

    mine = lax.dynamic_index_in_dim(active, myself, 1, keepdims=False)
    mine_cs = lax.dynamic_index_in_dim(col_slot, myself, 1, keepdims=False)
    mine_rs = lax.dynamic_index_in_dim(row_slot, myself, 1, keepdims=False)
    order = prefix_count(mine) - 1
    hit = mine[:, None, :] & (order[:, None, :] == jnp.arange(ACTIVE, dtype=jnp.int32)[None, :, None])
    present = jnp.any(hit, axis=-1)
    tile_ids = jnp.arange(per_holder, dtype=jnp.int32)
    slot_tile = jnp.sum(jnp.where(hit, tile_ids[None, None, :], 0), axis=-1)
    slot_cs = jnp.sum(jnp.where(hit, mine_cs[:, None, :], 0), axis=-1)
    slot_rs = jnp.sum(jnp.where(hit, mine_rs[:, None, :], 0), axis=-1)
    row_mask = present[..., None] & (slot_rs[..., None] == jnp.arange(2, dtype=jnp.int32))

    owner_node = jnp.arange(devices, dtype=jnp.int32)[None, :] * per_owner + owner_slot

    solved_rows = []
    latest = None
    for current in range(LEVELS):
        residue = jnp.sum(jnp.where(owner_at[current][:, :, None], rhs - update, 0.0), axis=1)
        if latest is not None:
            coming_prev, targets_prev = latest
            pick_rows = (owner_node[current][:, None] == targets_prev[None, :]).astype(jnp.float32)
            residue = residue - jnp.dot(pick_rows, coming_prev, precision=select_precision,
                                        preferred_element_type=jnp.float32)
            onehot = (node_ids[:, None] == targets_prev[None, :]).astype(jnp.float32)
            added = jnp.dot(onehot, coming_prev, precision=select_precision,
                            preferred_element_type=jnp.float32)
            update = update + added.reshape(devices, per_owner, block)
        gathered = a2a(residue)
        inverse = lax.dynamic_index_in_dim(diag_inverse, my_slot[current], 0, keepdims=False)
        solved = jnp.dot(gathered, inverse, precision=product_precision,
                         preferred_element_type=jnp.float32)
        returned = a2a(solved)
        solved_rows.append(returned)

        if current < tile_levels:
            carried = jnp.take(returned, col_owner[current].reshape(-1), axis=0,
                               mode="clip").reshape(devices, 2, block)
            blocks = a2a(carried)

            factors = jnp.take(factor_tiles, slot_tile[current], axis=0, mode="clip")
            sources = jnp.where(slot_cs[current][None, :, None] == 0,
                                blocks[:, 0:1, :], blocks[:, 1:2, :])
            terms = jnp.einsum("rtb,tbc->rtc", sources, factors, precision=product_precision,
                               preferred_element_type=jnp.float32)
            mask = row_mask[current]
            products = jnp.stack(
                [jnp.sum(jnp.where(mask[None, :, j, None], terms, 0.0), axis=1) for j in range(2)], axis=1)
            coming = a2a(products).reshape(devices * 2, block)
            latest = (coming, targets[current])
    solution = solved_rows[0][:, None, :]
    for current in range(1, LEVELS):
        solution = jnp.where(owner_at[current][:, :, None], solved_rows[current][:, None, :], solution)
    return solution.reshape(1, supernodes, block)


def solution(mesh):
    placed = (P("dev", None, None), P("dev", None, None), P("dev", None, None), P(), P(), P())
    return jax.shard_map(
        per_device, mesh=mesh, in_specs=placed, out_specs=P("dev", None, None), check_vma=False
    )
```

```python
import jax
import jax.numpy as jnp
from jax import lax
from jax.sharding import PartitionSpec as P

LEVELS = 5
ACTIVE = 4

product_precision = lax.Precision.HIGH
select_precision = lax.Precision.HIGHEST


def prefix_count(mask):
    m = mask.shape[-1]
    upto = jnp.arange(m)[:, None] <= jnp.arange(m)[None, :]
    return jnp.sum((upto & mask[..., :, None]).astype(jnp.int32), axis=-2)


def first_mask(mask):
    return mask & (prefix_count(mask) == 1)


def two_distinct(labels, active):
    l0 = jnp.sum(jnp.where(first_mask(active), labels[None], 0), axis=-1)
    other = active & (labels[None] != l0[..., None])
    l1 = jnp.sum(jnp.where(first_mask(other), labels[None], 0), axis=-1)
    ids = jnp.stack([l0, l1], axis=-1)
    valid = jnp.stack([jnp.any(active, axis=-1), jnp.any(other, axis=-1)], axis=-1)
    slot = (labels[None] != l0[..., None]).astype(jnp.int32)
    return ids, valid, slot


def a2a(x):
    return lax.all_to_all(x, "dev", split_axis=0, concat_axis=0, tiled=True)


def per_device(right_sides, diag_inverse, factor_tiles, node_level, tile_column, tile_row):
    devices = lax.axis_size("dev")
    myself = lax.axis_index("dev")
    per_owner = diag_inverse.shape[0]
    per_holder = factor_tiles.shape[0]
    block = factor_tiles.shape[1]
    supernodes = node_level.shape[0]
    tile_levels = LEVELS - 1

    rhs = right_sides[0].reshape(devices, per_owner, block)
    update = jnp.zeros_like(rhs)

    node_ids = jnp.arange(supernodes, dtype=jnp.int32)
    level_ids = jnp.arange(LEVELS, dtype=jnp.int32)
    tile_level = jnp.sum(jnp.where(tile_column[:, None] == node_ids[None, :], node_level[None, :], 0), axis=1)
    owner_levels = node_level.reshape(devices, per_owner)
    owner_at = owner_levels[None] == level_ids[:, None, None]
    my_owner_at = lax.dynamic_index_in_dim(owner_at, myself, 1, keepdims=False)
    my_slot = jnp.sum(jnp.where(my_owner_at, jnp.arange(per_owner, dtype=jnp.int32)[None], 0), axis=-1)
    owner_slot = jnp.sum(jnp.where(owner_at, jnp.arange(per_owner, dtype=jnp.int32)[None, None], 0), axis=-1)

    holder_levels = tile_level.reshape(devices, per_holder)
    active = holder_levels[None] == level_ids[:tile_levels, None, None]
    col_ids, col_valid, col_slot = two_distinct(tile_column.reshape(devices, per_holder), active)
    row_ids, row_valid, row_slot = two_distinct(tile_row.reshape(devices, per_holder), active)
    targets = jnp.where(row_valid, row_ids, -1).reshape(tile_levels, devices * 2)
    col_owner = col_ids // per_owner

    mine = lax.dynamic_index_in_dim(active, myself, 1, keepdims=False)
    mine_cs = lax.dynamic_index_in_dim(col_slot, myself, 1, keepdims=False)
    mine_rs = lax.dynamic_index_in_dim(row_slot, myself, 1, keepdims=False)
    order = prefix_count(mine) - 1
    hit = mine[:, None, :] & (order[:, None, :] == jnp.arange(ACTIVE, dtype=jnp.int32)[None, :, None])
    present = jnp.any(hit, axis=-1)
    tile_ids = jnp.arange(per_holder, dtype=jnp.int32)
    slot_tile = jnp.sum(jnp.where(hit, tile_ids[None, None, :], 0), axis=-1)
    slot_cs = jnp.sum(jnp.where(hit, mine_cs[:, None, :], 0), axis=-1)
    slot_rs = jnp.sum(jnp.where(hit, mine_rs[:, None, :], 0), axis=-1)
    two = jnp.arange(2, dtype=jnp.int32)
    combined = []
    for current in range(tile_levels):
        factors = jnp.take(factor_tiles, slot_tile[current], axis=0, mode="clip")
        where_to = (present[current][:, None, None] & (slot_cs[current][:, None, None] == two[None, :, None])
                    & (slot_rs[current][:, None, None] == two[None, None, :]))
        summed = jnp.sum(jnp.where(where_to[:, :, None, :, None], factors[:, None, :, None, :], 0.0), axis=0)
        combined.append(summed.reshape(2 * block, 2 * block))

    owner_node = jnp.arange(devices, dtype=jnp.int32)[None, :] * per_owner + owner_slot

    solved_rows = []
    latest = None
    for current in range(LEVELS):
        residue = jnp.sum(jnp.where(owner_at[current][:, :, None], rhs - update, 0.0), axis=1)
        if latest is not None:
            coming_prev, targets_prev = latest
            pick_rows = (owner_node[current][:, None] == targets_prev[None, :]).astype(jnp.float32)
            residue = residue - jnp.dot(pick_rows, coming_prev, precision=select_precision,
                                        preferred_element_type=jnp.float32)
            onehot = (node_ids[:, None] == targets_prev[None, :]).astype(jnp.float32)
            added = jnp.dot(onehot, coming_prev, precision=select_precision,
                            preferred_element_type=jnp.float32)
            update = update + added.reshape(devices, per_owner, block)
        gathered = a2a(residue)
        inverse = lax.dynamic_index_in_dim(diag_inverse, my_slot[current], 0, keepdims=False)
        solved = jnp.dot(gathered, inverse, precision=product_precision,
                         preferred_element_type=jnp.float32)
        returned = a2a(solved)
        solved_rows.append(returned)

        if current < tile_levels:
            carried = jnp.take(returned, col_owner[current], axis=0, mode="clip")
            blocks = a2a(carried)

            products = jnp.dot(blocks.reshape(devices, 2 * block), combined[current],
                               precision=product_precision,
                               preferred_element_type=jnp.float32).reshape(devices, 2, block)
            coming = a2a(products).reshape(devices * 2, block)
            latest = (coming, targets[current])
    solution = solved_rows[0][:, None, :]
    for current in range(1, LEVELS):
        solution = jnp.where(owner_at[current][:, :, None], solved_rows[current][:, None, :], solution)
    return solution.reshape(1, supernodes, block)


def solution(mesh):
    placed = (P("dev", None, None), P("dev", None, None), P("dev", None, None), P(), P(), P())
    return jax.shard_map(
        per_device, mesh=mesh, in_specs=placed, out_specs=P("dev", None, None), check_vma=False
    )
```

```python
import jax
import jax.numpy as jnp
from jax import lax
from jax.sharding import PartitionSpec as P

LEVELS = 5
ACTIVE = 4

product_precision = lax.Precision.HIGH
select_precision = lax.Precision.HIGHEST


def prefix_count(mask):
    m = mask.shape[-1]
    upto = jnp.arange(m)[:, None] <= jnp.arange(m)[None, :]
    return jnp.sum((upto & mask[..., :, None]).astype(jnp.int32), axis=-2)


def first_mask(mask):
    return mask & (prefix_count(mask) == 1)


def two_distinct(labels, active):
    l0 = jnp.sum(jnp.where(first_mask(active), labels[None], 0), axis=-1)
    other = active & (labels[None] != l0[..., None])
    l1 = jnp.sum(jnp.where(first_mask(other), labels[None], 0), axis=-1)
    ids = jnp.stack([l0, l1], axis=-1)
    valid = jnp.stack([jnp.any(active, axis=-1), jnp.any(other, axis=-1)], axis=-1)
    slot = (labels[None] != l0[..., None]).astype(jnp.int32)
    return ids, valid, slot


def a2a(x):
    return lax.all_to_all(x, "dev", split_axis=0, concat_axis=0, tiled=True)


def per_device(right_sides, diag_inverse, factor_tiles, node_level, tile_column, tile_row):
    devices = lax.axis_size("dev")
    myself = lax.axis_index("dev")
    per_owner = diag_inverse.shape[0]
    per_holder = factor_tiles.shape[0]
    block = factor_tiles.shape[1]
    supernodes = node_level.shape[0]
    tile_levels = LEVELS - 1

    rhs = right_sides[0].reshape(devices, per_owner, block)
    update = jnp.zeros_like(rhs)

    node_ids = jnp.arange(supernodes, dtype=jnp.int32)
    level_ids = jnp.arange(LEVELS, dtype=jnp.int32)
    tile_level = jnp.sum(jnp.where(tile_column[:, None] == node_ids[None, :], node_level[None, :], 0), axis=1)
    owner_levels = node_level.reshape(devices, per_owner)
    owner_at = owner_levels[None] == level_ids[:, None, None]
    my_owner_at = lax.dynamic_index_in_dim(owner_at, myself, 1, keepdims=False)
    my_slot = jnp.sum(jnp.where(my_owner_at, jnp.arange(per_owner, dtype=jnp.int32)[None], 0), axis=-1)
    owner_slot = jnp.sum(jnp.where(owner_at, jnp.arange(per_owner, dtype=jnp.int32)[None, None], 0), axis=-1)

    holder_levels = tile_level.reshape(devices, per_holder)
    active = holder_levels[None] == level_ids[:tile_levels, None, None]
    col_ids, col_valid, col_slot = two_distinct(tile_column.reshape(devices, per_holder), active)
    row_ids, row_valid, row_slot = two_distinct(tile_row.reshape(devices, per_holder), active)
    targets = jnp.where(row_valid, row_ids, -1).reshape(tile_levels, devices * 2)
    col_owner = col_ids // per_owner
    col_pick = (col_owner[..., None] == jnp.arange(devices, dtype=jnp.int32)).astype(jnp.float32)

    mine = lax.dynamic_index_in_dim(active, myself, 1, keepdims=False)
    mine_cs = lax.dynamic_index_in_dim(col_slot, myself, 1, keepdims=False)
    mine_rs = lax.dynamic_index_in_dim(row_slot, myself, 1, keepdims=False)
    order = prefix_count(mine) - 1
    hit = mine[:, None, :] & (order[:, None, :] == jnp.arange(ACTIVE, dtype=jnp.int32)[None, :, None])
    present = jnp.any(hit, axis=-1)
    tile_ids = jnp.arange(per_holder, dtype=jnp.int32)
    slot_tile = jnp.sum(jnp.where(hit, tile_ids[None, None, :], 0), axis=-1)
    slot_cs = jnp.sum(jnp.where(hit, mine_cs[:, None, :], 0), axis=-1)
    slot_rs = jnp.sum(jnp.where(hit, mine_rs[:, None, :], 0), axis=-1)
    row_mask = present[..., None] & (slot_rs[..., None] == jnp.arange(2, dtype=jnp.int32))

    owner_node = jnp.arange(devices, dtype=jnp.int32)[None, :] * per_owner + owner_slot

    solved_rows = []
    latest = None
    for current in range(LEVELS):
        residue = jnp.sum(jnp.where(owner_at[current][:, :, None], rhs - update, 0.0), axis=1)
        if latest is not None:
            coming_prev, targets_prev = latest
            pick_rows = (owner_node[current][:, None] == targets_prev[None, :]).astype(jnp.float32)
            residue = residue - jnp.dot(pick_rows, coming_prev, precision=select_precision,
                                        preferred_element_type=jnp.float32)
            onehot = (node_ids[:, None] == targets_prev[None, :]).astype(jnp.float32)
            added = jnp.dot(onehot, coming_prev, precision=select_precision,
                            preferred_element_type=jnp.float32)
            update = update + added.reshape(devices, per_owner, block)
        gathered = a2a(residue)
        inverse = lax.dynamic_index_in_dim(diag_inverse, my_slot[current], 0, keepdims=False)
        solved = jnp.dot(gathered, inverse, precision=product_precision,
                         preferred_element_type=jnp.float32)
        returned = a2a(solved)
        solved_rows.append(returned)

        if current < tile_levels:
            carried = jnp.einsum("hjo,ob->hjb", col_pick[current], returned, precision=select_precision,
                                 preferred_element_type=jnp.float32)
            blocks = a2a(carried)

            factors = jnp.take(factor_tiles, slot_tile[current], axis=0, mode="clip")
            sources = jnp.where(slot_cs[current][None, :, None] == 0,
                                blocks[:, 0:1, :], blocks[:, 1:2, :])
            terms = jnp.einsum("rtb,tbc->rtc", sources, factors, precision=product_precision,
                               preferred_element_type=jnp.float32)
            mask = row_mask[current]
            products = jnp.einsum("rtc,tj->rjc", terms, mask.astype(jnp.float32), precision=select_precision,
                                  preferred_element_type=jnp.float32)
            coming = a2a(products).reshape(devices * 2, block)
            latest = (coming, targets[current])
    solution = solved_rows[0][:, None, :]
    for current in range(1, LEVELS):
        solution = jnp.where(owner_at[current][:, :, None], solved_rows[current][:, None, :], solution)
    return solution.reshape(1, supernodes, block)


def solution(mesh):
    placed = (P("dev", None, None), P("dev", None, None), P("dev", None, None), P(), P(), P())
    return jax.shard_map(
        per_device, mesh=mesh, in_specs=placed, out_specs=P("dev", None, None), check_vma=False
    )
```

```python
import jax
import jax.numpy as jnp
from jax import lax
from jax.sharding import PartitionSpec as P

LEVELS = 5
ACTIVE = 4

product_precision = lax.Precision.HIGH
select_precision = lax.Precision.HIGHEST


def prefix_count(mask):
    m = mask.shape[-1]
    upto = jnp.arange(m)[:, None] <= jnp.arange(m)[None, :]
    return jnp.sum((upto & mask[..., :, None]).astype(jnp.int32), axis=-2)


def first_mask(mask):
    return mask & (prefix_count(mask) == 1)


def two_distinct(labels, active):
    l0 = jnp.sum(jnp.where(first_mask(active), labels[None], 0), axis=-1)
    other = active & (labels[None] != l0[..., None])
    l1 = jnp.sum(jnp.where(first_mask(other), labels[None], 0), axis=-1)
    ids = jnp.stack([l0, l1], axis=-1)
    valid = jnp.stack([jnp.any(active, axis=-1), jnp.any(other, axis=-1)], axis=-1)
    slot = (labels[None] != l0[..., None]).astype(jnp.int32)
    return ids, valid, slot


def a2a(x):
    return lax.all_to_all(x, "dev", split_axis=0, concat_axis=0, tiled=True)


def per_device(right_sides, diag_inverse, factor_tiles, node_level, tile_column, tile_row):
    devices = lax.axis_size("dev")
    myself = lax.axis_index("dev")
    per_owner = diag_inverse.shape[0]
    per_holder = factor_tiles.shape[0]
    block = factor_tiles.shape[1]
    supernodes = node_level.shape[0]
    tile_levels = LEVELS - 1

    rhs = right_sides[0].reshape(devices, per_owner, block)
    update = jnp.zeros_like(rhs)

    node_ids = jnp.arange(supernodes, dtype=jnp.int32)
    level_ids = jnp.arange(LEVELS, dtype=jnp.int32)
    tile_level = jnp.sum(jnp.where(tile_column[:, None] == node_ids[None, :], node_level[None, :], 0), axis=1)
    owner_levels = node_level.reshape(devices, per_owner)
    owner_at = owner_levels[None] == level_ids[:, None, None]
    my_owner_at = lax.dynamic_index_in_dim(owner_at, myself, 1, keepdims=False)
    my_slot = jnp.sum(jnp.where(my_owner_at, jnp.arange(per_owner, dtype=jnp.int32)[None], 0), axis=-1)
    owner_slot = jnp.sum(jnp.where(owner_at, jnp.arange(per_owner, dtype=jnp.int32)[None, None], 0), axis=-1)

    holder_levels = tile_level.reshape(devices, per_holder)
    active = holder_levels[None] == level_ids[:tile_levels, None, None]
    col_ids, col_valid, col_slot = two_distinct(tile_column.reshape(devices, per_holder), active)
    row_ids, row_valid, row_slot = two_distinct(tile_row.reshape(devices, per_holder), active)
    targets = jnp.where(row_valid, row_ids, -1).reshape(tile_levels, devices * 2)
    col_owner = col_ids // per_owner

    mine = lax.dynamic_index_in_dim(active, myself, 1, keepdims=False)
    mine_cs = lax.dynamic_index_in_dim(col_slot, myself, 1, keepdims=False)
    mine_rs = lax.dynamic_index_in_dim(row_slot, myself, 1, keepdims=False)
    order = prefix_count(mine) - 1
    hit = mine[:, None, :] & (order[:, None, :] == jnp.arange(ACTIVE, dtype=jnp.int32)[None, :, None])
    present = jnp.any(hit, axis=-1)
    tile_ids = jnp.arange(per_holder, dtype=jnp.int32)
    slot_tile = jnp.sum(jnp.where(hit, tile_ids[None, None, :], 0), axis=-1)
    slot_cs = jnp.sum(jnp.where(hit, mine_cs[:, None, :], 0), axis=-1)
    slot_rs = jnp.sum(jnp.where(hit, mine_rs[:, None, :], 0), axis=-1)
    row_mask = present[..., None] & (slot_rs[..., None] == jnp.arange(2, dtype=jnp.int32))

    owner_node = jnp.arange(devices, dtype=jnp.int32)[None, :] * per_owner + owner_slot

    solved_rows = []
    latest = None
    for current in range(LEVELS):
        residue = jnp.sum(jnp.where(owner_at[current][:, :, None], rhs - update, 0.0), axis=1)
        if latest is not None:
            coming_prev, targets_prev = latest
            pick_rows = (owner_node[current][:, None, None] == targets_prev[None]).astype(jnp.float32)
            residue = residue - jnp.einsum("ohj,hjb->ob", pick_rows, coming_prev, precision=select_precision,
                                           preferred_element_type=jnp.float32)
            onehot = (node_ids[:, None, None] == targets_prev[None]).astype(jnp.float32)
            added = jnp.einsum("shj,hjb->sb", onehot, coming_prev, precision=select_precision,
                               preferred_element_type=jnp.float32)
            update = update + added.reshape(devices, per_owner, block)
        gathered = a2a(residue)
        inverse = lax.dynamic_index_in_dim(diag_inverse, my_slot[current], 0, keepdims=False)
        solved = jnp.dot(gathered, inverse, precision=product_precision,
                         preferred_element_type=jnp.float32)
        returned = a2a(solved)
        solved_rows.append(returned)

        if current < tile_levels:
            carried = jnp.take(returned, col_owner[current].reshape(-1), axis=0,
                               mode="clip").reshape(devices, 2, block)
            blocks = a2a(carried)

            factors = jnp.take(factor_tiles, slot_tile[current], axis=0, mode="clip")
            sources = jnp.where(slot_cs[current][None, :, None] == 0,
                                blocks[:, 0:1, :], blocks[:, 1:2, :])
            terms = jnp.einsum("rtb,tbc->rtc", sources, factors, precision=product_precision,
                               preferred_element_type=jnp.float32)
            mask = row_mask[current]
            products = jnp.sum(jnp.where(mask[None, :, :, None], terms[:, :, None, :], 0.0), axis=1)
            coming = a2a(products)
            latest = (coming, targets[current].reshape(devices, 2))
    solution = solved_rows[0][:, None, :]
    for current in range(1, LEVELS - 1):
        solution = jnp.where(owner_at[current][:, :, None], solved_rows[current][:, None, :], solution)
    solution = lax.optimization_barrier(solution)
    last = LEVELS - 1
    solution = jnp.where(owner_at[last][:, :, None], solved_rows[last][:, None, :], solution)
    return solution.reshape(1, supernodes, block)


def solution(mesh):
    placed = (P("dev", None, None), P("dev", None, None), P("dev", None, None), P(), P(), P())
    return jax.shard_map(
        per_device, mesh=mesh, in_specs=placed, out_specs=P("dev", None, None), check_vma=False
    )
```

```python
import jax
import jax.numpy as jnp
from jax import lax
from jax.sharding import PartitionSpec as P

LEVELS = 5
ACTIVE = 4

product_precision = lax.Precision.HIGH
select_precision = lax.Precision.HIGHEST


def prefix_count(mask):
    m = mask.shape[-1]
    upto = jnp.arange(m)[:, None] <= jnp.arange(m)[None, :]
    return jnp.sum((upto & mask[..., :, None]).astype(jnp.int32), axis=-2)


def first_mask(mask):
    return mask & (prefix_count(mask) == 1)


def two_distinct(labels, active):
    l0 = jnp.sum(jnp.where(first_mask(active), labels[None], 0), axis=-1)
    other = active & (labels[None] != l0[..., None])
    l1 = jnp.sum(jnp.where(first_mask(other), labels[None], 0), axis=-1)
    ids = jnp.stack([l0, l1], axis=-1)
    valid = jnp.stack([jnp.any(active, axis=-1), jnp.any(other, axis=-1)], axis=-1)
    slot = (labels[None] != l0[..., None]).astype(jnp.int32)
    return ids, valid, slot


def a2a(x):
    return lax.all_to_all(x, "dev", split_axis=0, concat_axis=0, tiled=True)


def per_device(right_sides, diag_inverse, factor_tiles, node_level, tile_column, tile_row):
    devices = lax.axis_size("dev")
    myself = lax.axis_index("dev")
    per_owner = diag_inverse.shape[0]
    per_holder = factor_tiles.shape[0]
    block = factor_tiles.shape[1]
    supernodes = node_level.shape[0]
    tile_levels = LEVELS - 1

    rhs = right_sides[0].reshape(devices, per_owner, block)
    update = jnp.zeros_like(rhs)

    node_ids = jnp.arange(supernodes, dtype=jnp.int32)
    level_ids = jnp.arange(LEVELS, dtype=jnp.int32)
    tile_level = jnp.sum(jnp.where(tile_column[:, None] == node_ids[None, :], node_level[None, :], 0), axis=1)
    owner_levels = node_level.reshape(devices, per_owner)
    owner_at = owner_levels[None] == level_ids[:, None, None]
    my_owner_at = lax.dynamic_index_in_dim(owner_at, myself, 1, keepdims=False)
    my_slot = jnp.sum(jnp.where(my_owner_at, jnp.arange(per_owner, dtype=jnp.int32)[None], 0), axis=-1)
    owner_slot = jnp.sum(jnp.where(owner_at, jnp.arange(per_owner, dtype=jnp.int32)[None, None], 0), axis=-1)

    holder_levels = tile_level.reshape(devices, per_holder)
    active = holder_levels[None] == level_ids[:tile_levels, None, None]
    col_ids, col_valid, col_slot = two_distinct(tile_column.reshape(devices, per_holder), active)
    row_ids, row_valid, row_slot = two_distinct(tile_row.reshape(devices, per_holder), active)
    targets = jnp.where(row_valid, row_ids, -1).reshape(tile_levels, devices * 2)
    col_owner = col_ids // per_owner

    mine = lax.dynamic_index_in_dim(active, myself, 1, keepdims=False)
    mine_cs = lax.dynamic_index_in_dim(col_slot, myself, 1, keepdims=False)
    mine_rs = lax.dynamic_index_in_dim(row_slot, myself, 1, keepdims=False)
    order = prefix_count(mine) - 1
    hit = mine[:, None, :] & (order[:, None, :] == jnp.arange(ACTIVE, dtype=jnp.int32)[None, :, None])
    present = jnp.any(hit, axis=-1)
    tile_ids = jnp.arange(per_holder, dtype=jnp.int32)
    slot_tile = jnp.sum(jnp.where(hit, tile_ids[None, None, :], 0), axis=-1)
    slot_cs = jnp.sum(jnp.where(hit, mine_cs[:, None, :], 0), axis=-1)
    slot_rs = jnp.sum(jnp.where(hit, mine_rs[:, None, :], 0), axis=-1)
    row_mask = present[..., None] & (slot_rs[..., None] == jnp.arange(2, dtype=jnp.int32))

    owner_node = jnp.arange(devices, dtype=jnp.int32)[None, :] * per_owner + owner_slot

    solved_rows = []
    latest = None
    for current in range(LEVELS):
        residue = jnp.sum(jnp.where(owner_at[current][:, :, None], rhs - update, 0.0), axis=1)
        if latest is not None:
            coming_prev, targets_prev = latest
            pick_rows = (owner_node[current][:, None] == targets_prev[None, :]).astype(jnp.float32)
            residue = residue - jnp.dot(pick_rows, coming_prev, precision=select_precision,
                                        preferred_element_type=jnp.float32)
            onehot = (node_ids[:, None] == targets_prev[None, :]).astype(jnp.float32)
            added = jnp.dot(onehot, coming_prev, precision=select_precision,
                            preferred_element_type=jnp.float32)
            update = update + added.reshape(devices, per_owner, block)
        gathered = a2a(residue)
        inverse = lax.dynamic_index_in_dim(diag_inverse, my_slot[current], 0, keepdims=False)
        solved = jnp.dot(gathered, inverse, precision=product_precision,
                         preferred_element_type=jnp.float32)
        returned = a2a(solved)
        solved_rows.append(returned)

        if current < tile_levels:
            carried = jnp.take(returned, col_owner[current].reshape(-1), axis=0,
                               mode="clip").reshape(devices, 2, block)
            blocks = a2a(carried)

            factors = jnp.take(factor_tiles, slot_tile[current], axis=0, mode="clip")
            mask = row_mask[current]
            cs = slot_cs[current]
            quads = [[jnp.sum(jnp.where((mask[:, j] & (cs == c))[:, None, None], factors, 0.0), axis=0)
                      for j in range(2)] for c in range(2)]
            combined = jnp.concatenate([jnp.concatenate(row, axis=1) for row in quads], axis=0)
            products = jnp.dot(blocks.reshape(devices, 2 * block), combined, precision=product_precision,
                               preferred_element_type=jnp.float32).reshape(devices, 2, block)
            coming = a2a(products).reshape(devices * 2, block)
            latest = (coming, targets[current])
    solution = solved_rows[0][:, None, :]
    for current in range(1, LEVELS):
        solution = jnp.where(owner_at[current][:, :, None], solved_rows[current][:, None, :], solution)
    return solution.reshape(1, supernodes, block)


def solution(mesh):
    placed = (P("dev", None, None), P("dev", None, None), P("dev", None, None), P(), P(), P())
    return jax.shard_map(
        per_device, mesh=mesh, in_specs=placed, out_specs=P("dev", None, None), check_vma=False
    )
```

```python
import jax
import jax.numpy as jnp
from jax import lax
from jax.sharding import PartitionSpec as P

LEVELS = 5
ACTIVE = 4

product_precision = lax.Precision.HIGH
select_precision = lax.Precision.HIGHEST


def prefix_count(mask):
    m = mask.shape[-1]
    upto = jnp.arange(m)[:, None] <= jnp.arange(m)[None, :]
    return jnp.sum((upto & mask[..., :, None]).astype(jnp.int32), axis=-2)


def first_mask(mask):
    return mask & (prefix_count(mask) == 1)


def two_distinct(labels, active):
    l0 = jnp.sum(jnp.where(first_mask(active), labels[None], 0), axis=-1)
    other = active & (labels[None] != l0[..., None])
    l1 = jnp.sum(jnp.where(first_mask(other), labels[None], 0), axis=-1)
    ids = jnp.stack([l0, l1], axis=-1)
    valid = jnp.stack([jnp.any(active, axis=-1), jnp.any(other, axis=-1)], axis=-1)
    slot = (labels[None] != l0[..., None]).astype(jnp.int32)
    return ids, valid, slot


def a2a(x):
    return lax.all_to_all(x, "dev", split_axis=0, concat_axis=0, tiled=True)


def per_device(right_sides, diag_inverse, factor_tiles, node_level, tile_column, tile_row):
    devices = lax.axis_size("dev")
    myself = lax.axis_index("dev")
    per_owner = diag_inverse.shape[0]
    per_holder = factor_tiles.shape[0]
    block = factor_tiles.shape[1]
    supernodes = node_level.shape[0]
    tile_levels = LEVELS - 1

    rhs = right_sides[0].reshape(devices, per_owner, block)
    update = jnp.zeros_like(rhs)

    node_ids = jnp.arange(supernodes, dtype=jnp.int32)
    level_ids = jnp.arange(LEVELS, dtype=jnp.int32)
    tile_level = jnp.sum(jnp.where(tile_column[:, None] == node_ids[None, :], node_level[None, :], 0), axis=1)
    owner_levels = node_level.reshape(devices, per_owner)
    owner_at = owner_levels[None] == level_ids[:, None, None]
    my_owner_at = lax.dynamic_index_in_dim(owner_at, myself, 1, keepdims=False)
    my_slot = jnp.sum(jnp.where(my_owner_at, jnp.arange(per_owner, dtype=jnp.int32)[None], 0), axis=-1)
    owner_slot = jnp.sum(jnp.where(owner_at, jnp.arange(per_owner, dtype=jnp.int32)[None, None], 0), axis=-1)

    holder_levels = tile_level.reshape(devices, per_holder)
    active = holder_levels[None] == level_ids[:tile_levels, None, None]
    col_ids, col_valid, col_slot = two_distinct(tile_column.reshape(devices, per_holder), active)
    row_ids, row_valid, row_slot = two_distinct(tile_row.reshape(devices, per_holder), active)
    targets = jnp.where(row_valid, row_ids, -1).reshape(tile_levels, devices * 2)
    col_owner = col_ids // per_owner

    mine = lax.dynamic_index_in_dim(active, myself, 1, keepdims=False)
    mine_cs = lax.dynamic_index_in_dim(col_slot, myself, 1, keepdims=False)
    mine_rs = lax.dynamic_index_in_dim(row_slot, myself, 1, keepdims=False)
    order = prefix_count(mine) - 1
    hit = mine[:, None, :] & (order[:, None, :] == jnp.arange(ACTIVE, dtype=jnp.int32)[None, :, None])
    present = jnp.any(hit, axis=-1)
    tile_ids = jnp.arange(per_holder, dtype=jnp.int32)
    slot_tile = jnp.sum(jnp.where(hit, tile_ids[None, None, :], 0), axis=-1)
    slot_cs = jnp.sum(jnp.where(hit, mine_cs[:, None, :], 0), axis=-1)
    slot_rs = jnp.sum(jnp.where(hit, mine_rs[:, None, :], 0), axis=-1)
    row_mask = present[..., None] & (slot_rs[..., None] == jnp.arange(2, dtype=jnp.int32))

    owner_node = jnp.arange(devices, dtype=jnp.int32)[None, :] * per_owner + owner_slot

    def at_level(table, current):
        return lax.dynamic_index_in_dim(table, current, 0, keepdims=False)

    def residual(current, update, coming_prev, targets_prev):
        residue = jnp.sum(jnp.where(at_level(owner_at, current)[:, :, None], rhs - update, 0.0), axis=1)
        if coming_prev is not None:
            pick_rows = (at_level(owner_node, current)[:, None] == targets_prev[None, :]).astype(jnp.float32)
            residue = residue - jnp.dot(pick_rows, coming_prev, precision=select_precision,
                                        preferred_element_type=jnp.float32)
            onehot = (node_ids[:, None] == targets_prev[None, :]).astype(jnp.float32)
            added = jnp.dot(onehot, coming_prev, precision=select_precision,
                            preferred_element_type=jnp.float32)
            update = update + added.reshape(devices, per_owner, block)
        return residue, update

    def solve(current, residue):
        gathered = a2a(residue)
        inverse = lax.dynamic_index_in_dim(diag_inverse, at_level(my_slot, current), 0, keepdims=False)
        solved = jnp.dot(gathered, inverse, precision=product_precision,
                         preferred_element_type=jnp.float32)
        return a2a(solved)

    def tiles(current, returned):
        carried = jnp.take(returned, at_level(col_owner, current).reshape(-1), axis=0,
                           mode="clip").reshape(devices, 2, block)
        blocks = a2a(carried)
        factors = jnp.take(factor_tiles, at_level(slot_tile, current), axis=0, mode="clip")
        sources = jnp.where(at_level(slot_cs, current)[None, :, None] == 0,
                            blocks[:, 0:1, :], blocks[:, 1:2, :])
        terms = jnp.einsum("rtb,tbc->rtc", sources, factors, precision=product_precision,
                           preferred_element_type=jnp.float32)
        mask = at_level(row_mask, current)
        products = jnp.stack(
            [jnp.sum(jnp.where(mask[None, :, j, None], terms, 0.0), axis=1) for j in range(2)], axis=1)
        return a2a(products).reshape(devices * 2, block), at_level(targets, current)

    residue, update = residual(0, update, None, None)
    first = solve(0, residue)
    coming, coming_targets = tiles(0, first)

    def middle(current, carry):
        update, coming, coming_targets, kept = carry
        residue, update = residual(current, update, coming, coming_targets)
        returned = solve(current, residue)
        kept = lax.dynamic_update_index_in_dim(kept, returned, current - 1, 0)
        coming, coming_targets = tiles(current, returned)
        return update, coming, coming_targets, kept

    kept = jnp.zeros((tile_levels - 1, devices, block), jnp.float32)
    update, coming, coming_targets, kept = lax.fori_loop(
        1, tile_levels, middle, (update, coming, coming_targets, kept))
    residue, _ = residual(LEVELS - 1, update, coming, coming_targets)
    last = solve(LEVELS - 1, residue)

    solved_rows = [first] + [kept[i] for i in range(tile_levels - 1)] + [last]
    solution = solved_rows[0][:, None, :]
    for current in range(1, LEVELS):
        solution = jnp.where(owner_at[current][:, :, None], solved_rows[current][:, None, :], solution)
    return solution.reshape(1, supernodes, block)


def solution(mesh):
    placed = (P("dev", None, None), P("dev", None, None), P("dev", None, None), P(), P(), P())
    return jax.shard_map(
        per_device, mesh=mesh, in_specs=placed, out_specs=P("dev", None, None), check_vma=False
    )
```

```python
import jax
import jax.numpy as jnp
from jax import lax
from jax.sharding import PartitionSpec as P

LEVELS = 5
ACTIVE = 4

product_precision = lax.Precision.HIGH
select_precision = lax.Precision.HIGHEST


def prefix_count(mask):
    m = mask.shape[-1]
    upto = jnp.arange(m)[:, None] <= jnp.arange(m)[None, :]
    return jnp.sum((upto & mask[..., :, None]).astype(jnp.int32), axis=-2)


def first_mask(mask):
    return mask & (prefix_count(mask) == 1)


def two_distinct(labels, active):
    l0 = jnp.sum(jnp.where(first_mask(active), labels[None], 0), axis=-1)
    other = active & (labels[None] != l0[..., None])
    l1 = jnp.sum(jnp.where(first_mask(other), labels[None], 0), axis=-1)
    ids = jnp.stack([l0, l1], axis=-1)
    valid = jnp.stack([jnp.any(active, axis=-1), jnp.any(other, axis=-1)], axis=-1)
    slot = (labels[None] != l0[..., None]).astype(jnp.int32)
    return ids, valid, slot


def a2a(x):
    return lax.all_to_all(x, "dev", split_axis=0, concat_axis=0, tiled=True)


def per_device(right_sides, diag_inverse, factor_tiles, node_level, tile_column, tile_row):
    devices = lax.axis_size("dev")
    myself = lax.axis_index("dev")
    per_owner = diag_inverse.shape[0]
    per_holder = factor_tiles.shape[0]
    block = factor_tiles.shape[1]
    supernodes = node_level.shape[0]
    tile_levels = LEVELS - 1

    rhs = right_sides[0].reshape(devices, per_owner, block)
    update = jnp.zeros_like(rhs)

    node_ids = jnp.arange(supernodes, dtype=jnp.int32)
    level_ids = jnp.arange(LEVELS, dtype=jnp.int32)
    tile_level = jnp.sum(jnp.where(tile_column[:, None] == node_ids[None, :], node_level[None, :], 0), axis=1)
    owner_levels = node_level.reshape(devices, per_owner)
    owner_at = owner_levels[None] == level_ids[:, None, None]
    my_owner_at = lax.dynamic_index_in_dim(owner_at, myself, 1, keepdims=False)
    my_slot = jnp.sum(jnp.where(my_owner_at, jnp.arange(per_owner, dtype=jnp.int32)[None], 0), axis=-1)
    owner_slot = jnp.sum(jnp.where(owner_at, jnp.arange(per_owner, dtype=jnp.int32)[None, None], 0), axis=-1)

    holder_levels = tile_level.reshape(devices, per_holder)
    active = holder_levels[None] == level_ids[:tile_levels, None, None]
    col_ids, col_valid, col_slot = two_distinct(tile_column.reshape(devices, per_holder), active)
    row_ids, row_valid, row_slot = two_distinct(tile_row.reshape(devices, per_holder), active)
    targets = jnp.where(row_valid, row_ids, -1).reshape(tile_levels, devices * 2)
    col_owner = col_ids // per_owner

    mine = lax.dynamic_index_in_dim(active, myself, 1, keepdims=False)
    mine_cs = lax.dynamic_index_in_dim(col_slot, myself, 1, keepdims=False)
    mine_rs = lax.dynamic_index_in_dim(row_slot, myself, 1, keepdims=False)
    order = prefix_count(mine) - 1
    hit = mine[:, None, :] & (order[:, None, :] == jnp.arange(ACTIVE, dtype=jnp.int32)[None, :, None])
    present = jnp.any(hit, axis=-1)
    tile_ids = jnp.arange(per_holder, dtype=jnp.int32)
    slot_tile = jnp.sum(jnp.where(hit, tile_ids[None, None, :], 0), axis=-1)
    slot_cs = jnp.sum(jnp.where(hit, mine_cs[:, None, :], 0), axis=-1)
    slot_rs = jnp.sum(jnp.where(hit, mine_rs[:, None, :], 0), axis=-1)
    row_mask = present[..., None] & (slot_rs[..., None] == jnp.arange(2, dtype=jnp.int32))

    owner_node = jnp.arange(devices, dtype=jnp.int32)[None, :] * per_owner + owner_slot

    def at_level(table, current):
        return lax.dynamic_index_in_dim(table, current, 0, keepdims=False)

    def residual(current, update, coming_prev, targets_prev):
        residue = jnp.sum(jnp.where(at_level(owner_at, current)[:, :, None], rhs - update, 0.0), axis=1)
        if coming_prev is not None:
            pick_rows = (at_level(owner_node, current)[:, None] == targets_prev[None, :]).astype(jnp.float32)
            residue = residue - jnp.dot(pick_rows, coming_prev, precision=select_precision,
                                        preferred_element_type=jnp.float32)
            onehot = (node_ids[:, None] == targets_prev[None, :]).astype(jnp.float32)
            added = jnp.dot(onehot, coming_prev, precision=select_precision,
                            preferred_element_type=jnp.float32)
            update = update + added.reshape(devices, per_owner, block)
        return residue, update

    def solve(current, residue):
        gathered = a2a(residue)
        inverse = lax.dynamic_index_in_dim(diag_inverse, at_level(my_slot, current), 0, keepdims=False)
        solved = jnp.dot(gathered, inverse, precision=product_precision,
                         preferred_element_type=jnp.float32)
        return a2a(solved)

    def tiles(current, returned):
        carried = jnp.take(returned, at_level(col_owner, current).reshape(-1), axis=0,
                           mode="clip").reshape(devices, 2, block)
        blocks = a2a(carried)
        factors = jnp.take(factor_tiles, at_level(slot_tile, current), axis=0, mode="clip")
        sources = jnp.where(at_level(slot_cs, current)[None, :, None] == 0,
                            blocks[:, 0:1, :], blocks[:, 1:2, :])
        terms = jnp.einsum("rtb,tbc->rtc", sources, factors, precision=product_precision,
                           preferred_element_type=jnp.float32)
        mask = at_level(row_mask, current)
        products = jnp.stack(
            [jnp.sum(jnp.where(mask[None, :, j, None], terms, 0.0), axis=1) for j in range(2)], axis=1)
        return a2a(products).reshape(devices * 2, block), at_level(targets, current)

    def level(current, carry):
        update, coming, coming_targets, kept = carry
        residue, update = residual(current, update, coming, coming_targets)
        returned = solve(current, residue)
        kept = lax.dynamic_update_index_in_dim(kept, returned, current, 0)
        coming, coming_targets = tiles(current, returned)
        return update, coming, coming_targets, kept

    coming = jnp.zeros((devices * 2, block), jnp.float32)
    coming_targets = jnp.full((devices * 2,), -1, jnp.int32)
    kept = jnp.zeros((tile_levels, devices, block), jnp.float32)
    update, coming, coming_targets, kept = lax.fori_loop(
        0, tile_levels, level, (update, coming, coming_targets, kept))
    residue, _ = residual(LEVELS - 1, update, coming, coming_targets)
    last = solve(LEVELS - 1, residue)

    solved_rows = [kept[i] for i in range(tile_levels)] + [last]
    solution = solved_rows[0][:, None, :]
    for current in range(1, LEVELS):
        solution = jnp.where(owner_at[current][:, :, None], solved_rows[current][:, None, :], solution)
    return solution.reshape(1, supernodes, block)


def solution(mesh):
    placed = (P("dev", None, None), P("dev", None, None), P("dev", None, None), P(), P(), P())
    return jax.shard_map(
        per_device, mesh=mesh, in_specs=placed, out_specs=P("dev", None, None), check_vma=False
    )
```

```python
import jax
import jax.numpy as jnp
from jax import lax
from jax.sharding import PartitionSpec as P

LEVELS = 5
ACTIVE = 4

product_precision = lax.Precision.HIGH
select_precision = lax.Precision.HIGHEST


def prefix_count(mask):
    m = mask.shape[-1]
    upto = jnp.arange(m)[:, None] <= jnp.arange(m)[None, :]
    return jnp.sum((upto & mask[..., :, None]).astype(jnp.int32), axis=-2)


def first_mask(mask):
    return mask & (prefix_count(mask) == 1)


def two_distinct(labels, active):
    l0 = jnp.sum(jnp.where(first_mask(active), labels[None], 0), axis=-1)
    other = active & (labels[None] != l0[..., None])
    l1 = jnp.sum(jnp.where(first_mask(other), labels[None], 0), axis=-1)
    ids = jnp.stack([l0, l1], axis=-1)
    valid = jnp.stack([jnp.any(active, axis=-1), jnp.any(other, axis=-1)], axis=-1)
    slot = (labels[None] != l0[..., None]).astype(jnp.int32)
    return ids, valid, slot


def a2a(x):
    return lax.all_to_all(x, "dev", split_axis=0, concat_axis=0, tiled=True)


def per_device(right_sides, diag_inverse, factor_tiles, node_level, tile_column, tile_row):
    devices = lax.axis_size("dev")
    myself = lax.axis_index("dev")
    per_owner = diag_inverse.shape[0]
    per_holder = factor_tiles.shape[0]
    block = factor_tiles.shape[1]
    supernodes = node_level.shape[0]
    tile_levels = LEVELS - 1

    rhs = right_sides[0].reshape(devices, per_owner, block)
    update = jnp.zeros_like(rhs)

    node_ids = jnp.arange(supernodes, dtype=jnp.int32)
    level_ids = jnp.arange(LEVELS, dtype=jnp.int32)
    tile_level = jnp.sum(jnp.where(tile_column[:, None] == node_ids[None, :], node_level[None, :], 0), axis=1)
    owner_levels = node_level.reshape(devices, per_owner)
    owner_at = owner_levels[None] == level_ids[:, None, None]
    my_owner_at = lax.dynamic_index_in_dim(owner_at, myself, 1, keepdims=False)
    my_slot = jnp.sum(jnp.where(my_owner_at, jnp.arange(per_owner, dtype=jnp.int32)[None], 0), axis=-1)
    owner_slot = jnp.sum(jnp.where(owner_at, jnp.arange(per_owner, dtype=jnp.int32)[None, None], 0), axis=-1)

    holder_levels = tile_level.reshape(devices, per_holder)
    active = holder_levels[None] == level_ids[:tile_levels, None, None]
    col_ids, col_valid, col_slot = two_distinct(tile_column.reshape(devices, per_holder), active)
    row_ids, row_valid, row_slot = two_distinct(tile_row.reshape(devices, per_holder), active)
    targets = jnp.where(row_valid, row_ids, -1).reshape(tile_levels, devices * 2)
    col_owner = col_ids // per_owner

    mine = lax.dynamic_index_in_dim(active, myself, 1, keepdims=False)
    mine_cs = lax.dynamic_index_in_dim(col_slot, myself, 1, keepdims=False)
    mine_rs = lax.dynamic_index_in_dim(row_slot, myself, 1, keepdims=False)
    order = prefix_count(mine) - 1
    hit = mine[:, None, :] & (order[:, None, :] == jnp.arange(ACTIVE, dtype=jnp.int32)[None, :, None])
    present = jnp.any(hit, axis=-1)
    tile_ids = jnp.arange(per_holder, dtype=jnp.int32)
    slot_tile = jnp.sum(jnp.where(hit, tile_ids[None, None, :], 0), axis=-1)
    slot_cs = jnp.sum(jnp.where(hit, mine_cs[:, None, :], 0), axis=-1)
    slot_rs = jnp.sum(jnp.where(hit, mine_rs[:, None, :], 0), axis=-1)
    row_mask = present[..., None] & (slot_rs[..., None] == jnp.arange(2, dtype=jnp.int32))

    owner_node = jnp.arange(devices, dtype=jnp.int32)[None, :] * per_owner + owner_slot

    def at_level(table, current):
        return lax.dynamic_index_in_dim(table, current, 0, keepdims=False)

    def residual(current, update, coming_prev, targets_prev):
        residue = jnp.sum(jnp.where(at_level(owner_at, current)[:, :, None], rhs - update, 0.0), axis=1)
        if coming_prev is not None:
            pick_rows = (at_level(owner_node, current)[:, None] == targets_prev[None, :]).astype(jnp.float32)
            residue = residue - jnp.dot(pick_rows, coming_prev, precision=select_precision,
                                        preferred_element_type=jnp.float32)
            onehot = (node_ids[:, None] == targets_prev[None, :]).astype(jnp.float32)
            added = jnp.dot(onehot, coming_prev, precision=select_precision,
                            preferred_element_type=jnp.float32)
            update = update + added.reshape(devices, per_owner, block)
        return residue, update

    def solve(current, residue):
        gathered = a2a(residue)
        inverse = lax.dynamic_index_in_dim(diag_inverse, at_level(my_slot, current), 0, keepdims=False)
        solved = jnp.dot(gathered, inverse, precision=product_precision,
                         preferred_element_type=jnp.float32)
        return a2a(solved)

    def tiles(current, returned):
        carried = jnp.take(returned, at_level(col_owner, current).reshape(-1), axis=0,
                           mode="clip").reshape(devices, 2, block)
        blocks = a2a(carried)
        factors = jnp.take(factor_tiles, at_level(slot_tile, current), axis=0, mode="clip")
        sources = jnp.where(at_level(slot_cs, current)[None, :, None] == 0,
                            blocks[:, 0:1, :], blocks[:, 1:2, :])
        terms = jnp.einsum("rtb,tbc->rtc", sources, factors, precision=product_precision,
                           preferred_element_type=jnp.float32)
        mask = at_level(row_mask, current)
        products = jnp.stack(
            [jnp.sum(jnp.where(mask[None, :, j, None], terms, 0.0), axis=1) for j in range(2)], axis=1)
        return a2a(products).reshape(devices * 2, block), at_level(targets, current)

    residue, update = residual(0, update, None, None)
    first = solve(0, residue)
    kept = jnp.zeros((LEVELS, devices, block), jnp.float32)
    kept = lax.dynamic_update_index_in_dim(kept, first, 0, 0)

    def step(current, carry):
        update, returned, kept = carry
        coming, coming_targets = tiles(current, returned)
        residue, update = residual(current + 1, update, coming, coming_targets)
        returned = solve(current + 1, residue)
        kept = lax.dynamic_update_index_in_dim(kept, returned, current + 1, 0)
        return update, returned, kept

    update, _, kept = lax.fori_loop(0, tile_levels, step, (update, first, kept))
    solved_rows = [kept[i] for i in range(LEVELS)]
    solution = solved_rows[0][:, None, :]
    for current in range(1, LEVELS):
        solution = jnp.where(owner_at[current][:, :, None], solved_rows[current][:, None, :], solution)
    return solution.reshape(1, supernodes, block)


def solution(mesh):
    placed = (P("dev", None, None), P("dev", None, None), P("dev", None, None), P(), P(), P())
    return jax.shard_map(
        per_device, mesh=mesh, in_specs=placed, out_specs=P("dev", None, None), check_vma=False
    )
```

```python
import jax
import jax.numpy as jnp
from jax import lax
from jax.sharding import PartitionSpec as P

LEVELS = 5
ACTIVE = 4

product_precision = lax.Precision.HIGH
select_precision = lax.Precision.HIGHEST


def prefix_count(mask):
    m = mask.shape[-1]
    upto = jnp.arange(m)[:, None] <= jnp.arange(m)[None, :]
    return jnp.sum((upto & mask[..., :, None]).astype(jnp.int32), axis=-2)


def first_mask(mask):
    return mask & (prefix_count(mask) == 1)


def two_distinct(labels, active):
    l0 = jnp.sum(jnp.where(first_mask(active), labels[None], 0), axis=-1)
    other = active & (labels[None] != l0[..., None])
    l1 = jnp.sum(jnp.where(first_mask(other), labels[None], 0), axis=-1)
    ids = jnp.stack([l0, l1], axis=-1)
    valid = jnp.stack([jnp.any(active, axis=-1), jnp.any(other, axis=-1)], axis=-1)
    slot = (labels[None] != l0[..., None]).astype(jnp.int32)
    return ids, valid, slot


def a2a(x):
    return lax.all_to_all(x, "dev", split_axis=0, concat_axis=0, tiled=True)


def per_device(right_sides, diag_inverse, factor_tiles, node_level, tile_column, tile_row):
    devices = lax.axis_size("dev")
    myself = lax.axis_index("dev")
    per_owner = diag_inverse.shape[0]
    per_holder = factor_tiles.shape[0]
    block = factor_tiles.shape[1]
    supernodes = node_level.shape[0]
    tile_levels = LEVELS - 1

    rhs = right_sides[0].reshape(devices, per_owner, block)
    update = jnp.zeros_like(rhs)

    node_ids = jnp.arange(supernodes, dtype=jnp.int32)
    level_ids = jnp.arange(LEVELS, dtype=jnp.int32)
    tile_level = jnp.sum(jnp.where(tile_column[:, None] == node_ids[None, :], node_level[None, :], 0), axis=1)
    owner_levels = node_level.reshape(devices, per_owner)
    owner_at = owner_levels[None] == level_ids[:, None, None]
    my_owner_at = lax.dynamic_index_in_dim(owner_at, myself, 1, keepdims=False)
    my_slot = jnp.sum(jnp.where(my_owner_at, jnp.arange(per_owner, dtype=jnp.int32)[None], 0), axis=-1)
    owner_slot = jnp.sum(jnp.where(owner_at, jnp.arange(per_owner, dtype=jnp.int32)[None, None], 0), axis=-1)

    holder_levels = tile_level.reshape(devices, per_holder)
    active = holder_levels[None] == level_ids[:tile_levels, None, None]
    col_ids, col_valid, col_slot = two_distinct(tile_column.reshape(devices, per_holder), active)
    row_ids, row_valid, row_slot = two_distinct(tile_row.reshape(devices, per_holder), active)
    targets = jnp.where(row_valid, row_ids, -1).reshape(tile_levels, devices * 2)
    col_owner = col_ids // per_owner

    mine = lax.dynamic_index_in_dim(active, myself, 1, keepdims=False)
    mine_cs = lax.dynamic_index_in_dim(col_slot, myself, 1, keepdims=False)
    mine_rs = lax.dynamic_index_in_dim(row_slot, myself, 1, keepdims=False)
    order = prefix_count(mine) - 1
    hit = mine[:, None, :] & (order[:, None, :] == jnp.arange(ACTIVE, dtype=jnp.int32)[None, :, None])
    present = jnp.any(hit, axis=-1)
    tile_ids = jnp.arange(per_holder, dtype=jnp.int32)
    slot_tile = jnp.sum(jnp.where(hit, tile_ids[None, None, :], 0), axis=-1)
    slot_cs = jnp.sum(jnp.where(hit, mine_cs[:, None, :], 0), axis=-1)
    slot_rs = jnp.sum(jnp.where(hit, mine_rs[:, None, :], 0), axis=-1)
    row_mask = present[..., None] & (slot_rs[..., None] == jnp.arange(2, dtype=jnp.int32))

    owner_node = jnp.arange(devices, dtype=jnp.int32)[None, :] * per_owner + owner_slot

    def at_level(table, current):
        return lax.dynamic_index_in_dim(table, current, 0, keepdims=False)

    def residual(current, update, coming_prev, targets_prev):
        residue = jnp.sum(jnp.where(at_level(owner_at, current)[:, :, None], rhs - update, 0.0), axis=1)
        if coming_prev is not None:
            pick_rows = (at_level(owner_node, current)[:, None] == targets_prev[None, :]).astype(jnp.float32)
            residue = residue - jnp.dot(pick_rows, coming_prev, precision=select_precision,
                                        preferred_element_type=jnp.float32)
            onehot = (node_ids[:, None] == targets_prev[None, :]).astype(jnp.float32)
            added = jnp.dot(onehot, coming_prev, precision=select_precision,
                            preferred_element_type=jnp.float32)
            update = update + added.reshape(devices, per_owner, block)
        return residue, update

    def solve(current, residue):
        gathered = a2a(residue)
        inverse = lax.dynamic_index_in_dim(diag_inverse, at_level(my_slot, current), 0, keepdims=False)
        solved = jnp.dot(gathered, inverse, precision=product_precision,
                         preferred_element_type=jnp.float32)
        return a2a(solved)

    def tiles(current, returned):
        carried = jnp.take(returned, at_level(col_owner, current).reshape(-1), axis=0,
                           mode="clip").reshape(devices, 2, block)
        blocks = a2a(carried)
        factors = jnp.take(factor_tiles, at_level(slot_tile, current), axis=0, mode="clip")
        sources = jnp.where(at_level(slot_cs, current)[None, :, None] == 0,
                            blocks[:, 0:1, :], blocks[:, 1:2, :])
        terms = jnp.einsum("rtb,tbc->rtc", sources, factors, precision=product_precision,
                           preferred_element_type=jnp.float32)
        mask = at_level(row_mask, current)
        products = jnp.stack(
            [jnp.sum(jnp.where(mask[None, :, j, None], terms, 0.0), axis=1) for j in range(2)], axis=1)
        return a2a(products).reshape(devices * 2, block), at_level(targets, current)

    residue, update = residual(0, update, None, None)
    first = solve(0, residue)
    coming, coming_targets = tiles(0, first)

    def middle(current, carry):
        update, coming, coming_targets, solution = carry
        residue, update = residual(current, update, coming, coming_targets)
        returned = solve(current, residue)
        solution = jnp.where(at_level(owner_at, current)[:, :, None], returned[:, None, :], solution)
        coming, coming_targets = tiles(current, returned)
        return update, coming, coming_targets, solution

    solution = jnp.broadcast_to(first[:, None, :], (devices, per_owner, block))
    update, coming, coming_targets, solution = lax.fori_loop(
        1, tile_levels, middle, (update, coming, coming_targets, solution))
    residue, _ = residual(LEVELS - 1, update, coming, coming_targets)
    last = solve(LEVELS - 1, residue)
    solution = jnp.where(owner_at[LEVELS - 1][:, :, None], last[:, None, :], solution)
    return solution.reshape(1, supernodes, block)


def solution(mesh):
    placed = (P("dev", None, None), P("dev", None, None), P("dev", None, None), P(), P(), P())
    return jax.shard_map(
        per_device, mesh=mesh, in_specs=placed, out_specs=P("dev", None, None), check_vma=False
    )
```

```python
import jax
import jax.numpy as jnp
from jax import lax
from jax.sharding import PartitionSpec as P

LEVELS = 5
ACTIVE = 4

product_precision = lax.Precision.HIGH
select_precision = lax.Precision.HIGH


def prefix_count(mask):
    m = mask.shape[-1]
    upto = jnp.arange(m)[:, None] <= jnp.arange(m)[None, :]
    return jnp.sum((upto & mask[..., :, None]).astype(jnp.int32), axis=-2)


def first_mask(mask):
    return mask & (prefix_count(mask) == 1)


def two_distinct(labels, active):
    l0 = jnp.sum(jnp.where(first_mask(active), labels[None], 0), axis=-1)
    other = active & (labels[None] != l0[..., None])
    l1 = jnp.sum(jnp.where(first_mask(other), labels[None], 0), axis=-1)
    ids = jnp.stack([l0, l1], axis=-1)
    valid = jnp.stack([jnp.any(active, axis=-1), jnp.any(other, axis=-1)], axis=-1)
    slot = (labels[None] != l0[..., None]).astype(jnp.int32)
    return ids, valid, slot


def a2a(x):
    return lax.all_to_all(x, "dev", split_axis=0, concat_axis=0, tiled=True)


def per_device(right_sides, diag_inverse, factor_tiles, node_level, tile_column, tile_row):
    devices = lax.axis_size("dev")
    myself = lax.axis_index("dev")
    per_owner = diag_inverse.shape[0]
    per_holder = factor_tiles.shape[0]
    block = factor_tiles.shape[1]
    supernodes = node_level.shape[0]
    tile_levels = LEVELS - 1

    rhs = right_sides[0].reshape(devices, per_owner, block)
    update = jnp.zeros_like(rhs)

    node_ids = jnp.arange(supernodes, dtype=jnp.int32)
    level_ids = jnp.arange(LEVELS, dtype=jnp.int32)
    tile_level = jnp.sum(jnp.where(tile_column[:, None] == node_ids[None, :], node_level[None, :], 0), axis=1)
    owner_levels = node_level.reshape(devices, per_owner)
    owner_at = owner_levels[None] == level_ids[:, None, None]
    my_owner_at = lax.dynamic_index_in_dim(owner_at, myself, 1, keepdims=False)
    my_slot = jnp.sum(jnp.where(my_owner_at, jnp.arange(per_owner, dtype=jnp.int32)[None], 0), axis=-1)
    owner_slot = jnp.sum(jnp.where(owner_at, jnp.arange(per_owner, dtype=jnp.int32)[None, None], 0), axis=-1)

    holder_levels = tile_level.reshape(devices, per_holder)
    active = holder_levels[None] == level_ids[:tile_levels, None, None]
    col_ids, col_valid, col_slot = two_distinct(tile_column.reshape(devices, per_holder), active)
    row_ids, row_valid, row_slot = two_distinct(tile_row.reshape(devices, per_holder), active)
    targets = jnp.where(row_valid, row_ids, -1).reshape(tile_levels, devices * 2)
    col_owner = col_ids // per_owner

    mine = lax.dynamic_index_in_dim(active, myself, 1, keepdims=False)
    mine_cs = lax.dynamic_index_in_dim(col_slot, myself, 1, keepdims=False)
    mine_rs = lax.dynamic_index_in_dim(row_slot, myself, 1, keepdims=False)
    order = prefix_count(mine) - 1
    hit = mine[:, None, :] & (order[:, None, :] == jnp.arange(ACTIVE, dtype=jnp.int32)[None, :, None])
    present = jnp.any(hit, axis=-1)
    tile_ids = jnp.arange(per_holder, dtype=jnp.int32)
    slot_tile = jnp.sum(jnp.where(hit, tile_ids[None, None, :], 0), axis=-1)
    slot_cs = jnp.sum(jnp.where(hit, mine_cs[:, None, :], 0), axis=-1)
    slot_rs = jnp.sum(jnp.where(hit, mine_rs[:, None, :], 0), axis=-1)
    row_mask = present[..., None] & (slot_rs[..., None] == jnp.arange(2, dtype=jnp.int32))

    owner_node = jnp.arange(devices, dtype=jnp.int32)[None, :] * per_owner + owner_slot

    def at_level(table, current):
        return lax.dynamic_index_in_dim(table, current, 0, keepdims=False)

    def residual(current, update, coming_prev, targets_prev):
        residue = jnp.sum(jnp.where(at_level(owner_at, current)[:, :, None], rhs - update, 0.0), axis=1)
        if coming_prev is not None:
            pick_rows = (at_level(owner_node, current)[:, None] == targets_prev[None, :]).astype(jnp.float32)
            residue = residue - jnp.dot(pick_rows, coming_prev, precision=select_precision,
                                        preferred_element_type=jnp.float32)
            onehot = (node_ids[:, None] == targets_prev[None, :]).astype(jnp.float32)
            added = jnp.dot(onehot, coming_prev, precision=select_precision,
                            preferred_element_type=jnp.float32)
            update = update + added.reshape(devices, per_owner, block)
        return residue, update

    def solve(current, residue):
        gathered = a2a(residue)
        inverse = lax.dynamic_index_in_dim(diag_inverse, at_level(my_slot, current), 0, keepdims=False)
        solved = jnp.dot(gathered, inverse, precision=product_precision,
                         preferred_element_type=jnp.float32)
        return a2a(solved)

    def tiles(current, returned):
        carried = jnp.take(returned, at_level(col_owner, current).reshape(-1), axis=0,
                           mode="clip").reshape(devices, 2, block)
        blocks = a2a(carried)
        factors = jnp.take(factor_tiles, at_level(slot_tile, current), axis=0, mode="clip")
        sources = jnp.where(at_level(slot_cs, current)[None, :, None] == 0,
                            blocks[:, 0:1, :], blocks[:, 1:2, :])
        terms = jnp.einsum("rtb,tbc->rtc", sources, factors, precision=product_precision,
                           preferred_element_type=jnp.float32)
        mask = at_level(row_mask, current)
        products = jnp.stack(
            [jnp.sum(jnp.where(mask[None, :, j, None], terms, 0.0), axis=1) for j in range(2)], axis=1)
        return a2a(products).reshape(devices * 2, block), at_level(targets, current)

    residue, update = residual(0, update, None, None)
    first = solve(0, residue)
    coming, coming_targets = tiles(0, first)

    def middle(current, carry):
        update, coming, coming_targets, solution = carry
        residue, update = residual(current, update, coming, coming_targets)
        returned = solve(current, residue)
        solution = jnp.where(at_level(owner_at, current)[:, :, None], returned[:, None, :], solution)
        coming, coming_targets = tiles(current, returned)
        return update, coming, coming_targets, solution

    solution = jnp.broadcast_to(first[:, None, :], (devices, per_owner, block))
    update, coming, coming_targets, solution = lax.fori_loop(
        1, tile_levels, middle, (update, coming, coming_targets, solution))
    residue, _ = residual(LEVELS - 1, update, coming, coming_targets)
    last = solve(LEVELS - 1, residue)
    solution = jnp.where(owner_at[LEVELS - 1][:, :, None], last[:, None, :], solution)
    return solution.reshape(1, supernodes, block)


def solution(mesh):
    placed = (P("dev", None, None), P("dev", None, None), P("dev", None, None), P(), P(), P())
    return jax.shard_map(
        per_device, mesh=mesh, in_specs=placed, out_specs=P("dev", None, None), check_vma=False
    )
```

```python
import jax
import jax.numpy as jnp
from jax import lax
from jax.sharding import PartitionSpec as P

LEVELS = 5
ACTIVE = 4

product_precision = lax.Precision.HIGH
select_precision = lax.Precision.HIGHEST


def prefix_count(mask):
    m = mask.shape[-1]
    upto = jnp.arange(m)[:, None] <= jnp.arange(m)[None, :]
    return jnp.sum((upto & mask[..., :, None]).astype(jnp.int32), axis=-2)


def first_mask(mask):
    return mask & (prefix_count(mask) == 1)


def two_distinct(labels, active):
    l0 = jnp.sum(jnp.where(first_mask(active), labels[None], 0), axis=-1)
    other = active & (labels[None] != l0[..., None])
    l1 = jnp.sum(jnp.where(first_mask(other), labels[None], 0), axis=-1)
    ids = jnp.stack([l0, l1], axis=-1)
    valid = jnp.stack([jnp.any(active, axis=-1), jnp.any(other, axis=-1)], axis=-1)
    slot = (labels[None] != l0[..., None]).astype(jnp.int32)
    return ids, valid, slot


def a2a(x):
    return lax.all_to_all(x, "dev", split_axis=0, concat_axis=0, tiled=True)


def per_device(right_sides, diag_inverse, factor_tiles, node_level, tile_column, tile_row):
    devices = lax.axis_size("dev")
    myself = lax.axis_index("dev")
    per_owner = diag_inverse.shape[0]
    per_holder = factor_tiles.shape[0]
    block = factor_tiles.shape[1]
    supernodes = node_level.shape[0]
    tile_levels = LEVELS - 1

    rhs = right_sides[0].reshape(devices, per_owner, block)
    update = jnp.zeros_like(rhs)

    node_ids = jnp.arange(supernodes, dtype=jnp.int32)
    level_ids = jnp.arange(LEVELS, dtype=jnp.int32)
    tile_level = jnp.sum(jnp.where(tile_column[:, None] == node_ids[None, :], node_level[None, :], 0), axis=1)
    owner_levels = node_level.reshape(devices, per_owner)
    owner_at = owner_levels[None] == level_ids[:, None, None]
    my_owner_at = lax.dynamic_index_in_dim(owner_at, myself, 1, keepdims=False)
    my_slot = jnp.sum(jnp.where(my_owner_at, jnp.arange(per_owner, dtype=jnp.int32)[None], 0), axis=-1)
    owner_slot = jnp.sum(jnp.where(owner_at, jnp.arange(per_owner, dtype=jnp.int32)[None, None], 0), axis=-1)

    holder_levels = tile_level.reshape(devices, per_holder)
    active = holder_levels[None] == level_ids[:tile_levels, None, None]
    col_ids, col_valid, col_slot = two_distinct(tile_column.reshape(devices, per_holder), active)
    row_ids, row_valid, row_slot = two_distinct(tile_row.reshape(devices, per_holder), active)
    targets = jnp.where(row_valid, row_ids, -1).reshape(tile_levels, devices * 2)
    col_owner = col_ids // per_owner

    mine = lax.dynamic_index_in_dim(active, myself, 1, keepdims=False)
    mine_cs = lax.dynamic_index_in_dim(col_slot, myself, 1, keepdims=False)
    mine_rs = lax.dynamic_index_in_dim(row_slot, myself, 1, keepdims=False)
    order = prefix_count(mine) - 1
    hit = mine[:, None, :] & (order[:, None, :] == jnp.arange(ACTIVE, dtype=jnp.int32)[None, :, None])
    present = jnp.any(hit, axis=-1)
    tile_ids = jnp.arange(per_holder, dtype=jnp.int32)
    slot_tile = jnp.sum(jnp.where(hit, tile_ids[None, None, :], 0), axis=-1)
    slot_cs = jnp.sum(jnp.where(hit, mine_cs[:, None, :], 0), axis=-1)
    slot_rs = jnp.sum(jnp.where(hit, mine_rs[:, None, :], 0), axis=-1)
    row_mask = present[..., None] & (slot_rs[..., None] == jnp.arange(2, dtype=jnp.int32))

    owner_node = jnp.arange(devices, dtype=jnp.int32)[None, :] * per_owner + owner_slot

    def at_level(table, current):
        return lax.dynamic_index_in_dim(table, current, 0, keepdims=False)

    def residual(current, update, coming_prev, targets_prev):
        residue = jnp.sum(jnp.where(at_level(owner_at, current)[:, :, None], rhs - update, 0.0), axis=1)
        if coming_prev is not None:
            pick_rows = (at_level(owner_node, current)[:, None] == targets_prev[None, :]).astype(jnp.float32)
            residue = residue - jnp.dot(pick_rows, coming_prev, precision=select_precision,
                                        preferred_element_type=jnp.float32)
            onehot = (node_ids[:, None] == targets_prev[None, :]).astype(jnp.float32)
            added = jnp.dot(onehot, coming_prev, precision=select_precision,
                            preferred_element_type=jnp.float32)
            update = update + added.reshape(devices, per_owner, block)
        return residue, update

    def solve(current, residue):
        gathered = a2a(residue)
        inverse = lax.dynamic_index_in_dim(diag_inverse, at_level(my_slot, current), 0, keepdims=False)
        solved = jnp.dot(gathered, inverse, precision=product_precision,
                         preferred_element_type=jnp.float32)
        return a2a(solved)

    def tiles(current, returned):
        carried = jnp.take(returned, at_level(col_owner, current).reshape(-1), axis=0,
                           mode="clip").reshape(devices, 2, block)
        blocks = a2a(carried)
        factors = jnp.take(factor_tiles, at_level(slot_tile, current), axis=0, mode="clip")
        sources = jnp.where(at_level(slot_cs, current)[None, :, None] == 0,
                            blocks[:, 0:1, :], blocks[:, 1:2, :])
        terms = jnp.einsum("rtb,tbc->rtc", sources, factors, precision=product_precision,
                           preferred_element_type=jnp.float32)
        mask = at_level(row_mask, current)
        products = jnp.stack(
            [jnp.sum(jnp.where(mask[None, :, j, None], terms, 0.0), axis=1) for j in range(2)], axis=1)
        return a2a(products).reshape(devices * 2, block), at_level(targets, current)

    residue, update = residual(0, update, None, None)
    first = solve(0, residue)
    coming, coming_targets = tiles(0, first)

    def middle(current, carry):
        update, coming, coming_targets, solution = carry
        residue, update = residual(current, update, coming, coming_targets)
        returned = solve(current, residue)
        solution = jnp.where(at_level(row_at, current)[:, None], jnp.repeat(returned, per_owner, axis=0), solution)
        coming, coming_targets = tiles(current, returned)
        return update, coming, coming_targets, solution

    row_at = owner_at.reshape(LEVELS, supernodes)
    solution = jnp.repeat(first, per_owner, axis=0)
    update, coming, coming_targets, solution = lax.fori_loop(
        1, tile_levels, middle, (update, coming, coming_targets, solution))
    residue, _ = residual(LEVELS - 1, update, coming, coming_targets)
    last = solve(LEVELS - 1, residue)
    solution = jnp.where(row_at[LEVELS - 1][:, None], jnp.repeat(last, per_owner, axis=0), solution)
    return solution.reshape(1, supernodes, block)


def solution(mesh):
    placed = (P("dev", None, None), P("dev", None, None), P("dev", None, None), P(), P(), P())
    return jax.shard_map(
        per_device, mesh=mesh, in_specs=placed, out_specs=P("dev", None, None), check_vma=False
    )
```
